32 devices in a mesh: groups: 2 (over y), gx: 4 (over z), gy: 2 (over x), gz: 2 (over core).
Axes of the slice: x: 2, y: 2, z: 4, core: 2. Of those that a mesh axis runs over, the one named last changes fastest.
Arguments:
- coarse: bfloat16 [64, 16, 1024], P(('groups', 'gx'), ('gy', 'gz')), parts along dimension 0, may hold values from -6 to 6
- coarse_mask: int32 [64, 16, 16], P(('groups', 'gx'), ('gy', 'gz')), parts along dimension 0, may hold values 0 or 1
- brick_live: int32 [8, 2, 2], P(('groups', 'gx'), 'gy', 'gz'), parts along dimension 0, may hold values 0 or 1
- field: bfloat16 [128, 32, 2048], P(('groups', 'gx'), 'gy', 'gz'), parts along dimension 0, may hold values from -6 to 6
- coarse_weight: bfloat16 [64, 1728], replicated, may hold values from -0.15625 to 0.15625
- fine_weight_a: bfloat16 [64, 1728], replicated, may hold values from -0.15625 to 0.15625
- fine_weight_b: bfloat16 [64, 1728], replicated, may hold values from -0.15625 to 0.15625
- mod_weight: bfloat16 [64, 128], replicated, may hold values from -0.75 to 0.75
Outputs:
- decoded: bfloat16 [128, 32, 2048], P(('groups', 'gx'), 'gy', 'gz'), parts along dimension 0
The draws below stay inside these ranges and needn't reach their ends.
There are 2 independent parts, one for each index of `groups`. The reference program is written for one: setup_inputs(seed, part) draws one part's arguments, and reference() takes and returns one part's arrays. A program takes and returns all parts, laid end to end along the dimension named above; an argument that names none is the same for every part. Nothing has to cross between parts.
All inputs are finite; a program needn't handle non-finite values. No bound on the sum of `coarse_mask` or of `brick_live` on one device may be relied on, other than what follows from the above.
Results may differ from the reference program's by a relative error of at most 0.0057.
Values may be sent and summed in bfloat16 or wider, within the bound.
No kernel may reach another device: no remote copies, remote signals or barrier semaphores. Data moves between devices by JAX's collectives and lax.ppermute only.
A program may use at most 64 MiB of HBM per device.

```python
import jax
import jax.numpy as jnp
from jax import lax

C = 64
BRICK = 16
BZ_DEV = 1
NCX = 32
NCY = 16
NCZ = 16
NFX = 64
NFY = 32
NFZ = 32
N_GX = 4
N_GY = 2
N_GZ = 2


def with_ends(entries, key, low, top_value):
    shape = entries.shape
    place = [jax.random.randint(jax.random.fold_in(key, axis), (), 0, shape[axis]) for axis in range(len(shape))]
    entries = entries.at[tuple(place)].set(low)
    longest = shape.index(max(shape))
    place[longest] = (place[longest] + 1) % shape[longest]
    return entries.at[tuple(place)].set(top_value)


def steps_of(key, extent, cuts, low, top_value):
    level = 1.0
    for position, parts in cuts:
        steps = jax.random.uniform(jax.random.fold_in(jax.random.fold_in(key, 6), position), (parts,), jnp.float32, low / len(cuts), top_value / len(cuts))
        level = level * jnp.repeat(jnp.exp(steps), extent[position] // parts).reshape((-1,) + (1,) * (len(extent) - 1 - position))
    return level


def centred(key, shape, width, reach, cuts=(), kind=jnp.bfloat16):
    factor_of = steps_of(key, shape, cuts, -0.22, 0.18) if cuts else 1.0
    array = jax.random.normal(key, shape, jnp.float32) * width * factor_of
    return jnp.minimum(jnp.maximum(array, -reach), reach).astype(kind)


def setup_inputs(seed: int = 0, part: int = 0) -> dict:
    arg_keys = jax.random.split(jax.random.key(seed), 9)
    part_splits = jax.random.split(jax.random.fold_in(arg_keys[8], part), 9)
    return {
        "coarse": centred(part_splits[0], (NCX, NCY, NCZ * C), 1.0, 6.0, ((0, 4), (1, 4))),
        "coarse_mask": with_ends((jax.random.randint(part_splits[1], (NCX, NCY, NCZ), 0, 4) < 3).astype(jnp.int32), jax.random.fold_in(part_splits[1], 1), 0, 1),
        "brick_live": with_ends((jax.random.randint(part_splits[2], (N_GX, N_GY, BZ_DEV * N_GZ), 0, 3) < 2).astype(jnp.int32), jax.random.fold_in(part_splits[2], 1), 0, 1),
        "field": centred(part_splits[3], (NFX, NFY, NFZ * C), 1.0, 6.0, ((0, 4), (1, 2), (2, 2))),
        "coarse_weight": centred(arg_keys[4], (C, 27 * C), (27 * C) ** -0.5, 0.15625),
        "fine_weight_a": centred(arg_keys[5], (C, 27 * C), (27 * C) ** -0.5, 0.15625),
        "fine_weight_b": centred(arg_keys[6], (C, 27 * C), (27 * C) ** -0.5, 0.15625),
        "mod_weight": centred(arg_keys[7], (C, 2 * C), C ** -0.5, 0.75),
    }


conv_layout = ("NDHWC", "DHWIO", "NDHWC")


def convolve(volume, weight):
    channels = weight.shape[0]
    kernel = weight.astype(jnp.float32).reshape(channels, 3, 3, 3, channels).transpose(1, 2, 3, 0, 4)
    result = lax.conv_general_dilated(volume.astype(jnp.float32)[None], kernel, (1, 1, 1), "SAME", dimension_numbers=conv_layout, precision=lax.Precision.HIGHEST)
    return result[0]


def cell_mask(live, edge):
    return jnp.repeat(jnp.repeat(jnp.repeat(live, edge, axis=0), edge, axis=1), edge, axis=2)


def reference(coarse, coarse_mask, brick_live, field, coarse_weight, fine_weight_a, fine_weight_b, mod_weight):
    coarse_cells = coarse.reshape(NCX, NCY, NCZ, C)
    activity = convolve(coarse_cells, coarse_weight)
    keep = coarse_mask.astype(jnp.float32)[..., None]
    hidden = ((coarse_cells.astype(jnp.float32) + jax.nn.silu(activity)) * keep).astype(jnp.bfloat16)
    upsampled = jnp.repeat(jnp.repeat(jnp.repeat(hidden, 2, axis=0), 2, axis=1), 2, axis=2)
    live_cells = cell_mask(brick_live, BRICK)
    fine_input = upsampled * live_cells.astype(jnp.bfloat16)[..., None]
    live_float = live_cells.astype(jnp.float32)[..., None]
    gates = jax.nn.sigmoid(jnp.dot(field.reshape(-1, C), mod_weight, preferred_element_type=jnp.float32))
    gates = gates.reshape(NFX, NFY, NFZ, 2 * C)
    first_act = convolve(fine_input, fine_weight_a)
    level_one = (fine_input.astype(jnp.float32) + live_float * jax.nn.silu(first_act) * gates[..., :C]).astype(jnp.bfloat16)
    second_act = convolve(level_one, fine_weight_b)
    result = (level_one.astype(jnp.float32) + live_float * jax.nn.silu(second_act) * gates[..., C:]).astype(jnp.bfloat16)
    return result.reshape(NFX, NFY, NFZ * C)
```

```python
import jax
import jax.numpy as jnp
from jax import lax
from jax.sharding import PartitionSpec as P

conv_layout = ("NDHWC", "DHWIO", "NDHWC")


def convolve(padded, weight):
    channels = weight.shape[0]
    kernel = weight.reshape(channels, 3, 3, 3, channels).transpose(1, 2, 3, 0, 4)
    result = lax.conv_general_dilated(
        padded[None],
        kernel,
        (1, 1, 1),
        "VALID",
        dimension_numbers=conv_layout,
        preferred_element_type=jnp.float32,
    )
    return result[0]


def shift_pairs(count, up):
    if up:
        return [(k, k + 1) for k in range(count - 1)]
    return [(k + 1, k) for k in range(count - 1)]


def grow(cells, axis, dim, width):
    count = lax.axis_size(axis)
    size = cells.shape[dim]
    head = lax.slice_in_dim(cells, 0, width, axis=dim)
    tail = lax.slice_in_dim(cells, size - width, size, axis=dim)
    low = lax.ppermute(tail, axis, shift_pairs(count, True))
    high = lax.ppermute(head, axis, shift_pairs(count, False))
    return jnp.concatenate([low, cells, high], axis=dim)


def doubled(volume):
    size_x, size_y, size_z, channels = volume.shape
    spread = jnp.broadcast_to(
        volume[:, None, :, None, :, None, :], (size_x, 2, size_y, 2, size_z, 2, channels)
    )
    return spread.reshape(2 * size_x, 2 * size_y, 2 * size_z, channels)


def body(
    coarse, coarse_mask, brick_live, field, coarse_weight, fine_weight_a, fine_weight_b, mod_weight
):
    channels = coarse_weight.shape[0]
    rows_x, rows_y, flat_z = coarse.shape
    cells_z = flat_z // channels
    edge = field.shape[0]
    half = edge // 2
    assert lax.axis_size("gz") == 2 and rows_x == half and 2 * rows_y == half
    lanes = 128
    zside = lax.axis_index("gz")
    first = zside == 0
    live = brick_live.reshape(())

    extra = jnp.concatenate(
        [
            coarse_mask.astype(jnp.bfloat16),
            jnp.broadcast_to(live.astype(jnp.bfloat16), (rows_x, rows_y, 1)),
            jnp.zeros((rows_x, rows_y, lanes - cells_z - 1), jnp.bfloat16),
        ],
        axis=2,
    )
    mine = jnp.concatenate([coarse, extra], axis=2)
    theirs = lax.ppermute(mine, "gz", [(0, 1), (1, 0)])
    column = jnp.where(first, jnp.concatenate([mine, theirs], 1), jnp.concatenate([theirs, mine], 1))
    live_other = theirs[0, 0, flat_z + cells_z]
    live_mine = live.astype(jnp.bfloat16)
    live_low = jnp.where(first, live_mine, live_other)
    live_high = jnp.where(first, live_other, live_mine)
    zcoarse = lax.broadcasted_iota(jnp.int32, (1, 1, cells_z), 2)
    live_z = jnp.where(zcoarse < half, live_low, live_high)
    keep = column[:, :, flat_z : flat_z + cells_z] * live_z
    packed = jnp.concatenate(
        [
            column[:, :, :flat_z],
            keep,
            jnp.zeros((rows_x, 2 * rows_y, lanes - cells_z), jnp.bfloat16),
        ],
        axis=2,
    )

    region = grow(grow(packed, "gy", 1, 2), "gx", 0, 2)
    size = region.shape[0]
    volume = region[:, :, :flat_z].reshape(size, size, cells_z, channels)
    volume = jnp.pad(volume, ((0, 0), (0, 0), (2, 2), (0, 0)))
    volume = lax.dynamic_slice_in_dim(volume, zside * half, half + 4, axis=2)
    keep = jnp.pad(region[:, :, flat_z : flat_z + cells_z], ((0, 0), (0, 0), (2, 2)))
    keep = lax.dynamic_slice_in_dim(keep, zside * half + 1, half + 2, axis=2)[1:-1, 1:-1]
    activity = convolve(volume, coarse_weight)
    centre = volume[1:-1, 1:-1, 1:-1].astype(jnp.float32)
    hidden = ((centre + jax.nn.silu(activity)) * keep[..., None].astype(jnp.float32)).astype(
        jnp.bfloat16
    )
    fine_input = doubled(hidden)

    product = jnp.dot(
        field.reshape(-1, channels), mod_weight, preferred_element_type=jnp.float32
    )
    gates = jax.nn.sigmoid(product).reshape(edge, edge, edge, 2 * channels) * live.astype(
        jnp.float32
    )
    gate_a = gates[..., :channels]
    gate_b = gates[..., channels:]
    face = jnp.where(first, gate_a[:, :, -1], gate_a[:, :, 0])
    face = lax.ppermute(face, "gz", [(0, 1), (1, 0)])[:, :, None]
    blank = jnp.zeros_like(face)
    gate_a = jnp.where(
        first,
        jnp.concatenate([blank, gate_a, face], 2),
        jnp.concatenate([face, gate_a, blank], 2),
    )
    gate_a = grow(grow(gate_a, "gy", 1, 1), "gx", 0, 1)

    first_act = convolve(fine_input, fine_weight_a)
    level_one = (
        fine_input[1:-1, 1:-1, 1:-1].astype(jnp.float32) + jax.nn.silu(first_act) * gate_a
    ).astype(jnp.bfloat16)
    second_act = convolve(level_one, fine_weight_b)
    result = (
        level_one[1:-1, 1:-1, 1:-1].astype(jnp.float32) + jax.nn.silu(second_act) * gate_b
    ).astype(jnp.bfloat16)
    return result.reshape(edge, edge, edge * channels)


def solution(mesh):
    in_specs = (
        P(("groups", "gx"), ("gy", "gz"), None),
        P(("groups", "gx"), ("gy", "gz"), None),
        P(("groups", "gx"), "gy", "gz"),
        P(("groups", "gx"), "gy", "gz"),
        P(),
        P(),
        P(),
        P(),
    )
    out_specs = P(("groups", "gx"), "gy", "gz")
    return jax.shard_map(body, mesh=mesh, in_specs=in_specs, out_specs=out_specs, check_vma=False)
```

```python
import jax
import jax.numpy as jnp
from jax import lax
from jax.experimental import pallas as pl
from jax.experimental.pallas import tpu as pltpu
from jax.sharding import PartitionSpec as P

conv_layout = ("NDHWC", "DHWIO", "NDHWC")

STRIDE = 24
ROWS_C = 112
ROWS_F = 488
ROWS_A = 432
ROWS_B = 384
ROWS_L = 440
LANES_F = 1408
LANES_A = 1280
LANES_B = 1024


def bands(weight):
    channels = weight.shape[0]
    cells = weight.astype(jnp.float32).reshape(channels, 3, 3, 3, channels)
    pick = (
        jnp.arange(6)[:, None, None] - jnp.arange(4)[None, :, None] == jnp.arange(3)[None, None, :]
    ).astype(jnp.float32)
    band = jnp.einsum("abd,ixydo->xyaibo", pick, cells, precision=lax.Precision.HIGHEST)
    return band.reshape(9, 6 * channels, 4 * channels).astype(jnp.bfloat16)


def silu(v):
    return v / (1.0 + jnp.exp(-v))


def fine_kernel(hid_ref, spread_ref, ga_ref, gb_ref, wa_ref, wb_ref, out_ref, fin_ref, lvl_ref):
    wide_c = hid_ref.shape[1]
    i = lax.broadcasted_iota(jnp.int32, (wide_c, LANES_F), 0)
    j = lax.broadcasted_iota(jnp.int32, (wide_c, LANES_F), 1)
    zup = (((i >> 6) == (j >> 7)) & ((i & 63) == (j & 63)) & (j < LANES_A)).astype(jnp.bfloat16)
    deep = jnp.dot(hid_ref[...], zup, preferred_element_type=jnp.float32).astype(jnp.bfloat16)
    fin_ref[...] = jnp.dot(spread_ref[...], deep, preferred_element_type=jnp.float32)
    r = lax.broadcasted_iota(jnp.int32, (384, 256), 0)
    c = lax.broadcasted_iota(jnp.int32, (384, 256), 1)
    shift = (r == c + 64).astype(jnp.bfloat16)
    lvl_ref[ROWS_A:, :] = jnp.zeros((ROWS_L - ROWS_A, LANES_A), jnp.float32)

    def conv(src, weights, rows, chunk):
        acc = jnp.zeros((rows, 256), jnp.float32)
        centre = None
        for t in range(9):
            dx, dy = divmod(t, 3)
            off = dx * STRIDE + dy
            a = src[off : off + rows, 256 * chunk : 256 * chunk + 384].astype(jnp.bfloat16)
            acc = acc + jnp.dot(a, weights[t], preferred_element_type=jnp.float32)
            if t == 4:
                centre = jnp.dot(a, shift, preferred_element_type=jnp.float32)
        return centre, acc

    for k in range(LANES_A // 256):
        centre, acc = conv(fin_ref, wa_ref, ROWS_A, k)
        lanes = slice(256 * k, 256 * k + 256)
        step = centre + silu(acc) * ga_ref[:, lanes]
        lvl_ref[:ROWS_A, lanes] = step.astype(jnp.bfloat16).astype(jnp.float32)
    for k in range(LANES_B // 256):
        centre, acc = conv(lvl_ref, wb_ref, ROWS_B, k)
        lanes = slice(256 * k, 256 * k + 256)
        out_ref[:, lanes] = (centre + silu(acc) * gb_ref[:, lanes]).astype(out_ref.dtype)


def fine_stage(hid, spread, gate_a, gate_b, band_a, band_b):
    return pl.pallas_call(
        fine_kernel,
        out_shape=jax.ShapeDtypeStruct((ROWS_B, LANES_B), jnp.bfloat16),
        scratch_shapes=[
            pltpu.VMEM((ROWS_F, LANES_F), jnp.float32),
            pltpu.VMEM((ROWS_L, LANES_A), jnp.float32),
        ],
    )(hid, spread, gate_a, gate_b, band_a, band_b)


def convolve(padded, weight):
    channels = weight.shape[0]
    kernel = weight.reshape(channels, 3, 3, 3, channels).transpose(1, 2, 3, 0, 4)
    result = lax.conv_general_dilated(
        padded[None],
        kernel,
        (1, 1, 1),
        "VALID",
        dimension_numbers=conv_layout,
        preferred_element_type=jnp.float32,
    )
    return result[0]


def shift_pairs(count, up):
    if up:
        return [(k, k + 1) for k in range(count - 1)]
    return [(k + 1, k) for k in range(count - 1)]


def grow(cells, axis, dim, width):
    count = lax.axis_size(axis)
    size = cells.shape[dim]
    head = lax.slice_in_dim(cells, 0, width, axis=dim)
    tail = lax.slice_in_dim(cells, size - width, size, axis=dim)
    low = lax.ppermute(tail, axis, shift_pairs(count, True))
    high = lax.ppermute(head, axis, shift_pairs(count, False))
    return jnp.concatenate([low, cells, high], axis=dim)


def body(
    coarse, coarse_mask, brick_live, field, coarse_weight, fine_weight_a, fine_weight_b, mod_weight
):
    channels = coarse_weight.shape[0]
    rows_x, rows_y, flat_z = coarse.shape
    cells_z = flat_z // channels
    edge = field.shape[0]
    half = edge // 2
    assert lax.axis_size("gz") == 2 and rows_x == half and 2 * rows_y == half
    lanes = 128
    zside = lax.axis_index("gz")
    first = zside == 0
    live = brick_live.reshape(())

    extra = jnp.concatenate(
        [
            coarse_mask.astype(jnp.bfloat16),
            jnp.broadcast_to(live.astype(jnp.bfloat16), (rows_x, rows_y, 1)),
            jnp.zeros((rows_x, rows_y, lanes - cells_z - 1), jnp.bfloat16),
        ],
        axis=2,
    )
    mine = jnp.concatenate([coarse, extra], axis=2)
    theirs = lax.ppermute(mine, "gz", [(0, 1), (1, 0)])
    column = jnp.where(first, jnp.concatenate([mine, theirs], 1), jnp.concatenate([theirs, mine], 1))
    live_other = theirs[0, 0, flat_z + cells_z]
    live_mine = live.astype(jnp.bfloat16)
    live_low = jnp.where(first, live_mine, live_other)
    live_high = jnp.where(first, live_other, live_mine)
    zcoarse = lax.broadcasted_iota(jnp.int32, (1, 1, cells_z), 2)
    live_z = jnp.where(zcoarse < half, live_low, live_high)
    keep = column[:, :, flat_z : flat_z + cells_z] * live_z
    packed = jnp.concatenate(
        [
            column[:, :, :flat_z],
            keep,
            jnp.zeros((rows_x, 2 * rows_y, lanes - cells_z), jnp.bfloat16),
        ],
        axis=2,
    )

    region = grow(grow(packed, "gy", 1, 2), "gx", 0, 2)
    size = region.shape[0]
    volume = region[:, :, :flat_z].reshape(size, size, cells_z, channels)
    volume = jnp.pad(volume, ((0, 0), (0, 0), (2, 2), (0, 0)))
    volume = lax.dynamic_slice_in_dim(volume, zside * half, half + 4, axis=2)
    keep = jnp.pad(region[:, :, flat_z : flat_z + cells_z], ((0, 0), (0, 0), (2, 2)))
    keep = lax.dynamic_slice_in_dim(keep, zside * half + 1, half + 2, axis=2)[1:-1, 1:-1]
    activity = convolve(volume, coarse_weight)
    centre = volume[1:-1, 1:-1, 1:-1].astype(jnp.float32)
    hidden = ((centre + jax.nn.silu(activity)) * keep[..., None].astype(jnp.float32)).astype(
        jnp.bfloat16
    )
    cells = hidden.shape[0] * hidden.shape[1]
    hid = jnp.pad(hidden.reshape(cells, -1), ((0, ROWS_C - cells), (0, 0)))

    eye = jnp.eye(edge, dtype=jnp.float32)
    flat_w = mod_weight.astype(jnp.float32)

    def gate(part):
        block = (eye[:, None, :, None] * part[None, :, None, :]).reshape(
            edge * channels, edge * channels
        )
        return jax.nn.sigmoid(
            jnp.einsum(
                "xyl,lm->xym", field, block.astype(jnp.bfloat16), preferred_element_type=jnp.float32
            )
        ) * live.astype(jnp.float32)

    gate_a = gate(flat_w[:, :channels])
    gate_b = gate(flat_w[:, channels:])
    width = edge * channels
    face = jnp.where(first, gate_a[:, :, width - channels :], gate_a[:, :, :channels])
    face = lax.ppermute(face, "gz", [(0, 1), (1, 0)])
    blank = jnp.zeros_like(face)
    gate_a = jnp.concatenate(
        [
            jnp.where(first, blank, face),
            gate_a,
            jnp.where(first, face, blank),
            jnp.zeros((edge, edge, 2 * channels), jnp.float32),
        ],
        axis=2,
    )
    gate_a = grow(grow(gate_a, "gy", 1, 1), "gx", 0, 1)
    gate_a = jnp.pad(gate_a, ((0, 0), (0, STRIDE - edge - 2), (0, 0))).reshape(-1, gate_a.shape[2])
    gate_b = jnp.pad(gate_b, ((0, 0), (0, STRIDE - edge), (0, 0))).reshape(-1, width)

    rows = jnp.arange(ROWS_F)
    fx, fy = rows // STRIDE, rows % STRIDE
    inside = (fx < edge + 4) & (fy < edge + 4)
    source = (fx // 2) * (half + 2) + fy // 2
    spread = (inside[:, None] & (source[:, None] == jnp.arange(ROWS_C)[None, :])).astype(
        jnp.bfloat16
    )
    out = fine_stage(hid, spread, gate_a, gate_b, bands(fine_weight_a), bands(fine_weight_b))
    return out.reshape(edge, STRIDE, width)[:, :edge]


def solution(mesh):
    in_specs = (
        P(("groups", "gx"), ("gy", "gz"), None),
        P(("groups", "gx"), ("gy", "gz"), None),
        P(("groups", "gx"), "gy", "gz"),
        P(("groups", "gx"), "gy", "gz"),
        P(),
        P(),
        P(),
        P(),
    )
    out_specs = P(("groups", "gx"), "gy", "gz")
    return jax.shard_map(body, mesh=mesh, in_specs=in_specs, out_specs=out_specs, check_vma=False)
```

```python
import jax
import jax.numpy as jnp
from jax import lax
from jax.experimental import pallas as pl
from jax.experimental.pallas import tpu as pltpu
from jax.sharding import PartitionSpec as P

conv_layout = ("NDHWC", "DHWIO", "NDHWC")

STRIDE = 24
ROWS_C = 112
ROWS_F = 488
ROWS_A = 432
ROWS_B = 384
ROWS_L = 440
LANES_F = 1408
LANES_A = 1280
LANES_B = 1024


def select(shape, rule):
    rows = lax.broadcasted_iota(jnp.int32, shape, 0)
    cols = lax.broadcasted_iota(jnp.int32, shape, 1)
    return rule(rows, cols)


def build_bands(w_ref, band_ref):
    rows_all = select((384, 64), lambda r, c: (r & 63) == c).astype(jnp.bfloat16)
    halves = [
        select((128, 256), lambda r, c, h=h: ((r >> 6) == h) & ((r & 63) == (c & 63))).astype(
            jnp.bfloat16
        )
        for h in range(2)
    ]
    for t in range(9):
        acc = jnp.zeros((384, 256), jnp.float32)
        for dz in range(3):
            d = 3 * t + dz
            block = w_ref[:, 128 * (d // 2) : 128 * (d // 2) + 128]
            spread = jnp.dot(block, halves[d % 2], preferred_element_type=jnp.float32)
            tall = jnp.dot(rows_all, spread.astype(jnp.bfloat16), preferred_element_type=jnp.float32)
            keep = select((384, 256), lambda r, c, dz=dz: (r >> 6) - (c >> 6) == dz)
            acc = acc + jnp.where(keep, tall, 0.0)
        band_ref[t] = acc.astype(jnp.bfloat16)


def gate_kernel(field_ref, mw_ref, live_ref, ga_ref, gb_ref):
    tiles = []
    for part in range(2):
        pick = select((128, 128), lambda r, c, p=part: ((r >> 6) == p) & ((r & 63) == (c & 63)))
        spread = jnp.dot(mw_ref[...], pick.astype(jnp.bfloat16), preferred_element_type=jnp.float32)
        rows_all = select((128, 64), lambda r, c: (r & 63) == c).astype(jnp.bfloat16)
        tall = jnp.dot(rows_all, spread.astype(jnp.bfloat16), preferred_element_type=jnp.float32)
        keep = select((128, 128), lambda r, c: (r >> 6) == (c >> 6))
        tiles.append(jnp.where(keep, tall, 0.0).astype(jnp.bfloat16))
    live = live_ref[...]
    for k in range(field_ref.shape[1] // 128):
        lanes = slice(128 * k, 128 * k + 128)
        x = field_ref[:, lanes]
        for tile, out in zip(tiles, (ga_ref, gb_ref)):
            v = jnp.dot(x, tile, preferred_element_type=jnp.float32)
            out[:, lanes] = live / (1.0 + jnp.exp(-v))


def gate_stage(field2d, mod_weight, live_row):
    shape = jax.ShapeDtypeStruct(field2d.shape, jnp.float32)
    return pl.pallas_call(gate_kernel, out_shape=(shape, shape))(field2d, mod_weight, live_row)


def silu(v):
    return v / (1.0 + jnp.exp(-v))


def fine_kernel(
    hid_ref, spread_ref, ga_ref, gb_ref, wa_raw, wb_raw, out_ref, fin_ref, lvl_ref, wa_ref, wb_ref
):
    build_bands(wa_raw, wa_ref)
    build_bands(wb_raw, wb_ref)
    wide_c = hid_ref.shape[1]
    i = lax.broadcasted_iota(jnp.int32, (wide_c, LANES_F), 0)
    j = lax.broadcasted_iota(jnp.int32, (wide_c, LANES_F), 1)
    zup = (((i >> 6) == (j >> 7)) & ((i & 63) == (j & 63)) & (j < LANES_A)).astype(jnp.bfloat16)
    deep = jnp.dot(hid_ref[...], zup, preferred_element_type=jnp.float32).astype(jnp.bfloat16)
    fin_ref[...] = jnp.dot(spread_ref[...], deep, preferred_element_type=jnp.float32)
    r = lax.broadcasted_iota(jnp.int32, (384, 256), 0)
    c = lax.broadcasted_iota(jnp.int32, (384, 256), 1)
    shift = (r == c + 64).astype(jnp.bfloat16)
    lvl_ref[ROWS_A:, :] = jnp.zeros((ROWS_L - ROWS_A, LANES_A), jnp.float32)

    def conv(src, weights, rows, chunk):
        acc = jnp.zeros((rows, 256), jnp.float32)
        centre = None
        for t in range(9):
            dx, dy = divmod(t, 3)
            off = dx * STRIDE + dy
            a = src[off : off + rows, 256 * chunk : 256 * chunk + 384].astype(jnp.bfloat16)
            acc = acc + jnp.dot(a, weights[t], preferred_element_type=jnp.float32)
            if t == 4:
                centre = jnp.dot(a, shift, preferred_element_type=jnp.float32)
        return centre, acc

    for k in range(LANES_A // 256):
        centre, acc = conv(fin_ref, wa_ref, ROWS_A, k)
        lanes = slice(256 * k, 256 * k + 256)
        step = centre + silu(acc) * ga_ref[:, lanes]
        lvl_ref[:ROWS_A, lanes] = step.astype(jnp.bfloat16).astype(jnp.float32)
    for k in range(LANES_B // 256):
        centre, acc = conv(lvl_ref, wb_ref, ROWS_B, k)
        lanes = slice(256 * k, 256 * k + 256)
        out_ref[:, lanes] = (centre + silu(acc) * gb_ref[:, lanes]).astype(out_ref.dtype)


def fine_stage(hid, spread, gate_a, gate_b, band_a, band_b):
    return pl.pallas_call(
        fine_kernel,
        out_shape=jax.ShapeDtypeStruct((ROWS_B, LANES_B), jnp.bfloat16),
        scratch_shapes=[
            pltpu.VMEM((ROWS_F, LANES_F), jnp.float32),
            pltpu.VMEM((ROWS_L, LANES_A), jnp.float32),
            pltpu.VMEM((9, 384, 256), jnp.bfloat16),
            pltpu.VMEM((9, 384, 256), jnp.bfloat16),
        ],
    )(hid, spread, gate_a, gate_b, band_a, band_b)


def convolve(padded, weight):
    channels = weight.shape[0]
    kernel = weight.reshape(channels, 3, 3, 3, channels).transpose(1, 2, 3, 0, 4)
    result = lax.conv_general_dilated(
        padded[None],
        kernel,
        (1, 1, 1),
        "VALID",
        dimension_numbers=conv_layout,
        preferred_element_type=jnp.float32,
    )
    return result[0]


def shift_pairs(count, up):
    if up:
        return [(k, k + 1) for k in range(count - 1)]
    return [(k + 1, k) for k in range(count - 1)]


def grow(cells, axis, dim, width):
    count = lax.axis_size(axis)
    size = cells.shape[dim]
    head = lax.slice_in_dim(cells, 0, width, axis=dim)
    tail = lax.slice_in_dim(cells, size - width, size, axis=dim)
    low = lax.ppermute(tail, axis, shift_pairs(count, True))
    high = lax.ppermute(head, axis, shift_pairs(count, False))
    return jnp.concatenate([low, cells, high], axis=dim)


def body(
    coarse, coarse_mask, brick_live, field, coarse_weight, fine_weight_a, fine_weight_b, mod_weight
):
    channels = coarse_weight.shape[0]
    rows_x, rows_y, flat_z = coarse.shape
    cells_z = flat_z // channels
    edge = field.shape[0]
    half = edge // 2
    assert lax.axis_size("gz") == 2 and rows_x == half and 2 * rows_y == half
    lanes = 128
    zside = lax.axis_index("gz")
    first = zside == 0
    live = brick_live.reshape(())

    extra = jnp.concatenate(
        [
            coarse_mask.astype(jnp.bfloat16),
            jnp.broadcast_to(live.astype(jnp.bfloat16), (rows_x, rows_y, 1)),
            jnp.zeros((rows_x, rows_y, lanes - cells_z - 1), jnp.bfloat16),
        ],
        axis=2,
    )
    mine = jnp.concatenate([coarse, extra], axis=2)
    theirs = lax.ppermute(mine, "gz", [(0, 1), (1, 0)])
    column = jnp.where(first, jnp.concatenate([mine, theirs], 1), jnp.concatenate([theirs, mine], 1))
    live_other = theirs[0, 0, flat_z + cells_z]
    live_mine = live.astype(jnp.bfloat16)
    live_low = jnp.where(first, live_mine, live_other)
    live_high = jnp.where(first, live_other, live_mine)
    zcoarse = lax.broadcasted_iota(jnp.int32, (1, 1, cells_z), 2)
    live_z = jnp.where(zcoarse < half, live_low, live_high)
    keep = column[:, :, flat_z : flat_z + cells_z] * live_z
    packed = jnp.concatenate(
        [
            column[:, :, :flat_z],
            keep,
            jnp.zeros((rows_x, 2 * rows_y, lanes - cells_z), jnp.bfloat16),
        ],
        axis=2,
    )

    region = grow(grow(packed, "gy", 1, 2), "gx", 0, 2)
    size = region.shape[0]
    volume = region[:, :, :flat_z].reshape(size, size, cells_z, channels)
    volume = jnp.pad(volume, ((0, 0), (0, 0), (2, 2), (0, 0)))
    volume = lax.dynamic_slice_in_dim(volume, zside * half, half + 4, axis=2)
    keep = jnp.pad(region[:, :, flat_z : flat_z + cells_z], ((0, 0), (0, 0), (2, 2)))
    keep = lax.dynamic_slice_in_dim(keep, zside * half + 1, half + 2, axis=2)[1:-1, 1:-1]
    activity = convolve(volume, coarse_weight)
    centre = volume[1:-1, 1:-1, 1:-1].astype(jnp.float32)
    hidden = ((centre + jax.nn.silu(activity)) * keep[..., None].astype(jnp.float32)).astype(
        jnp.bfloat16
    )
    cells = hidden.shape[0] * hidden.shape[1]
    hid = jnp.pad(hidden.reshape(cells, -1), ((0, ROWS_C - cells), (0, 0)))

    live_row = jnp.broadcast_to(live.astype(jnp.float32), (1, 128))
    gate_a, gate_b = gate_stage(field.reshape(edge * edge, -1), mod_weight, live_row)
    gate_a = gate_a.reshape(field.shape)
    gate_b = gate_b.reshape(field.shape)
    width = edge * channels
    face = jnp.where(first, gate_a[:, :, width - channels :], gate_a[:, :, :channels])
    face = lax.ppermute(face, "gz", [(0, 1), (1, 0)])
    blank = jnp.zeros_like(face)
    gate_a = jnp.concatenate(
        [
            jnp.where(first, blank, face),
            gate_a,
            jnp.where(first, face, blank),
            jnp.zeros((edge, edge, 2 * channels), jnp.float32),
        ],
        axis=2,
    )
    gate_a = grow(grow(gate_a, "gy", 1, 1), "gx", 0, 1)
    gate_a = jnp.pad(gate_a, ((0, 0), (0, STRIDE - edge - 2), (0, 0))).reshape(-1, gate_a.shape[2])
    gate_b = jnp.pad(gate_b, ((0, 0), (0, STRIDE - edge), (0, 0))).reshape(-1, width)

    rows = jnp.arange(ROWS_F)
    fx, fy = rows // STRIDE, rows % STRIDE
    inside = (fx < edge + 4) & (fy < edge + 4)
    source = (fx // 2) * (half + 2) + fy // 2
    spread = (inside[:, None] & (source[:, None] == jnp.arange(ROWS_C)[None, :])).astype(
        jnp.bfloat16
    )
    wide = ((0, 0), (0, 1792 - fine_weight_a.shape[1]))
    out = fine_stage(
        hid, spread, gate_a, gate_b, jnp.pad(fine_weight_a, wide), jnp.pad(fine_weight_b, wide)
    )
    return out.reshape(edge, STRIDE, width)[:, :edge]


def solution(mesh):
    in_specs = (
        P(("groups", "gx"), ("gy", "gz"), None),
        P(("groups", "gx"), ("gy", "gz"), None),
        P(("groups", "gx"), "gy", "gz"),
        P(("groups", "gx"), "gy", "gz"),
        P(),
        P(),
        P(),
        P(),
    )
    out_specs = P(("groups", "gx"), "gy", "gz")
    return jax.shard_map(body, mesh=mesh, in_specs=in_specs, out_specs=out_specs, check_vma=False)
```

```python
import jax
import jax.numpy as jnp
from jax import lax
from jax.experimental import pallas as pl
from jax.experimental.pallas import tpu as pltpu
from jax.sharding import PartitionSpec as P

conv_layout = ("NDHWC", "DHWIO", "NDHWC")

STRIDE = 24
ROWS_C = 112
ROWS_F = 488
ROWS_A = 432
ROWS_B = 384
ROWS_L = 440
LANES_F = 1408
LANES_A = 1280
LANES_B = 1024


def select(shape, rule):
    rows = lax.broadcasted_iota(jnp.int32, shape, 0)
    cols = lax.broadcasted_iota(jnp.int32, shape, 1)
    return rule(rows, cols)


def build_bands(w_ref, band_ref):
    rows_all = select((384, 64), lambda r, c: (r & 63) == c).astype(jnp.bfloat16)
    halves = [
        select((128, 256), lambda r, c, h=h: ((r >> 6) == h) & ((r & 63) == (c & 63))).astype(
            jnp.bfloat16
        )
        for h in range(2)
    ]
    for t in range(9):
        acc = jnp.zeros((384, 256), jnp.float32)
        for dz in range(3):
            d = 3 * t + dz
            block = w_ref[:, 128 * (d // 2) : 128 * (d // 2) + 128]
            spread = jnp.dot(block, halves[d % 2], preferred_element_type=jnp.float32)
            tall = jnp.dot(rows_all, spread.astype(jnp.bfloat16), preferred_element_type=jnp.float32)
            keep = select((384, 256), lambda r, c, dz=dz: (r >> 6) - (c >> 6) == dz)
            acc = acc + jnp.where(keep, tall, 0.0)
        band_ref[t] = acc.astype(jnp.bfloat16)


def gate_kernel(field_ref, mw_ref, live_ref, ga_ref, gb_ref):
    tiles = []
    for part in range(2):
        pick = select((128, 128), lambda r, c, p=part: ((r >> 6) == p) & ((r & 63) == (c & 63)))
        spread = jnp.dot(mw_ref[...], pick.astype(jnp.bfloat16), preferred_element_type=jnp.float32)
        rows_all = select((128, 64), lambda r, c: (r & 63) == c).astype(jnp.bfloat16)
        tall = jnp.dot(rows_all, spread.astype(jnp.bfloat16), preferred_element_type=jnp.float32)
        keep = select((128, 128), lambda r, c: (r >> 6) == (c >> 6))
        tiles.append(jnp.where(keep, tall, 0.0).astype(jnp.bfloat16))
    live = live_ref[...]
    for k in range(field_ref.shape[1] // 128):
        lanes = slice(128 * k, 128 * k + 128)
        x = field_ref[:, lanes]
        for tile, out in zip(tiles, (ga_ref, gb_ref)):
            v = jnp.dot(x, tile, preferred_element_type=jnp.float32)
            out[:, lanes] = live / (1.0 + jnp.exp(-v))


def gate_stage(field2d, mod_weight, live_row):
    shape = jax.ShapeDtypeStruct(field2d.shape, jnp.float32)
    return pl.pallas_call(gate_kernel, out_shape=(shape, shape))(field2d, mod_weight, live_row)


def silu(v):
    return v / (1.0 + jnp.exp(-v))


def fine_kernel(
    hid_ref, spread_ref, ga_ref, gb_ref, wa_raw, wb_raw, out_ref, fin_ref, lvl_ref, wa_ref, wb_ref
):
    build_bands(wa_raw, wa_ref)
    build_bands(wb_raw, wb_ref)
    wide_c = hid_ref.shape[1]
    i = lax.broadcasted_iota(jnp.int32, (wide_c, LANES_F), 0)
    j = lax.broadcasted_iota(jnp.int32, (wide_c, LANES_F), 1)
    zup = (((i >> 6) == (j >> 7)) & ((i & 63) == (j & 63)) & (j < LANES_A)).astype(jnp.bfloat16)
    deep = jnp.dot(hid_ref[...], zup, preferred_element_type=jnp.float32).astype(jnp.bfloat16)
    fin_ref[...] = jnp.dot(spread_ref[...], deep, preferred_element_type=jnp.float32)
    r = lax.broadcasted_iota(jnp.int32, (384, 256), 0)
    c = lax.broadcasted_iota(jnp.int32, (384, 256), 1)
    shift = (r == c + 64).astype(jnp.bfloat16)
    lvl_ref[ROWS_A:, :] = jnp.zeros((ROWS_L - ROWS_A, LANES_A), jnp.float32)

    def conv(src, weights, rows, chunk):
        acc = jnp.zeros((rows, 256), jnp.float32)
        centre = None
        for t in range(9):
            dx, dy = divmod(t, 3)
            off = dx * STRIDE + dy
            a = src[off : off + rows, 256 * chunk : 256 * chunk + 384].astype(jnp.bfloat16)
            acc = acc + jnp.dot(a, weights[t], preferred_element_type=jnp.float32)
            if t == 4:
                centre = jnp.dot(a, shift, preferred_element_type=jnp.float32)
        return centre, acc

    for k in range(LANES_A // 256):
        centre, acc = conv(fin_ref, wa_ref, ROWS_A, k)
        lanes = slice(256 * k, 256 * k + 256)
        step = centre + silu(acc) * ga_ref[:, lanes]
        lvl_ref[:ROWS_A, lanes] = step.astype(jnp.bfloat16).astype(jnp.float32)
    for k in range(LANES_B // 256):
        centre, acc = conv(lvl_ref, wb_ref, ROWS_B, k)
        lanes = slice(256 * k, 256 * k + 256)
        out_ref[:, lanes] = (centre + silu(acc) * gb_ref[:, lanes]).astype(out_ref.dtype)


def fine_stage(hid, spread, gate_a, gate_b, band_a, band_b):
    return pl.pallas_call(
        fine_kernel,
        out_shape=jax.ShapeDtypeStruct((ROWS_B, LANES_B), jnp.bfloat16),
        scratch_shapes=[
            pltpu.VMEM((ROWS_F, LANES_F), jnp.float32),
            pltpu.VMEM((ROWS_L, LANES_A), jnp.float32),
            pltpu.VMEM((9, 384, 256), jnp.bfloat16),
            pltpu.VMEM((9, 384, 256), jnp.bfloat16),
        ],
    )(hid, spread, gate_a, gate_b, band_a, band_b)


def convolve(padded, weight):
    channels = weight.shape[0]
    kernel = weight.reshape(channels, 3, 3, 3, channels).transpose(1, 2, 3, 0, 4)
    result = lax.conv_general_dilated(
        padded[None],
        kernel,
        (1, 1, 1),
        "VALID",
        dimension_numbers=conv_layout,
        preferred_element_type=jnp.float32,
    )
    return result[0]


def shift_pairs(count, up):
    if up:
        return [(k, k + 1) for k in range(count - 1)]
    return [(k + 1, k) for k in range(count - 1)]


def grow_both(cells, gate, axis, dim, widths):
    count = lax.axis_size(axis)
    lanes = gate.shape[-1]

    def ends(arr, width):
        size = arr.shape[dim]
        return lax.slice_in_dim(arr, 0, width, axis=dim), lax.slice_in_dim(arr, size - width, size, axis=dim)

    (cells_head, cells_tail), (gate_head, gate_tail) = ends(cells, widths[0]), ends(gate, widths[1])

    def pack(c, g):
        return jnp.concatenate([c.astype(jnp.float32).reshape(-1, lanes), g.reshape(-1, lanes)], 0)

    def unpack(m):
        split = cells_head.size // lanes
        return m[:split].reshape(cells_head.shape).astype(cells.dtype), m[split:].reshape(gate_head.shape)

    low = unpack(lax.ppermute(pack(cells_tail, gate_tail), axis, shift_pairs(count, True)))
    high = unpack(lax.ppermute(pack(cells_head, gate_head), axis, shift_pairs(count, False)))
    return (
        jnp.concatenate([low[0], cells, high[0]], axis=dim),
        jnp.concatenate([low[1], gate, high[1]], axis=dim),
    )


def grow(cells, axis, dim, width):
    count = lax.axis_size(axis)
    size = cells.shape[dim]
    head = lax.slice_in_dim(cells, 0, width, axis=dim)
    tail = lax.slice_in_dim(cells, size - width, size, axis=dim)
    low = lax.ppermute(tail, axis, shift_pairs(count, True))
    high = lax.ppermute(head, axis, shift_pairs(count, False))
    return jnp.concatenate([low, cells, high], axis=dim)


def body(
    coarse, coarse_mask, brick_live, field, coarse_weight, fine_weight_a, fine_weight_b, mod_weight
):
    channels = coarse_weight.shape[0]
    rows_x, rows_y, flat_z = coarse.shape
    cells_z = flat_z // channels
    edge = field.shape[0]
    half = edge // 2
    assert lax.axis_size("gz") == 2 and rows_x == half and 2 * rows_y == half
    lanes = 256
    zside = lax.axis_index("gz")
    first = zside == 0
    live = brick_live.reshape(())

    extra = jnp.concatenate(
        [
            coarse_mask.astype(jnp.bfloat16),
            jnp.broadcast_to(live.astype(jnp.bfloat16), (rows_x, rows_y, 1)),
            jnp.zeros((rows_x, rows_y, lanes - cells_z - 1), jnp.bfloat16),
        ],
        axis=2,
    )
    mine = jnp.concatenate([coarse, extra], axis=2)
    theirs = lax.ppermute(mine, "gz", [(0, 1), (1, 0)])
    column = jnp.where(first, jnp.concatenate([mine, theirs], 1), jnp.concatenate([theirs, mine], 1))
    live_other = theirs[0, 0, flat_z + cells_z]
    live_mine = live.astype(jnp.bfloat16)
    live_low = jnp.where(first, live_mine, live_other)
    live_high = jnp.where(first, live_other, live_mine)
    zcoarse = lax.broadcasted_iota(jnp.int32, (1, 1, cells_z), 2)
    live_z = jnp.where(zcoarse < half, live_low, live_high)
    keep = column[:, :, flat_z : flat_z + cells_z] * live_z
    packed = jnp.concatenate(
        [
            column[:, :, :flat_z],
            keep,
            jnp.zeros((rows_x, 2 * rows_y, lanes - cells_z), jnp.bfloat16),
        ],
        axis=2,
    )

    live_row = jnp.broadcast_to(live.astype(jnp.float32), (1, 128))
    gate_a, gate_b = gate_stage(field.reshape(edge * edge, -1), mod_weight, live_row)
    gate_a = gate_a.reshape(field.shape)
    gate_b = gate_b.reshape(field.shape)
    width = edge * channels
    face = jnp.where(first, gate_a[:, :, width - channels :], gate_a[:, :, :channels])
    face = lax.ppermute(face, "gz", [(0, 1), (1, 0)])
    blank = jnp.zeros_like(face)
    gate_a = jnp.concatenate(
        [
            jnp.where(first, blank, face),
            gate_a,
            jnp.where(first, face, blank),
            jnp.zeros((edge, edge, 2 * channels), jnp.float32),
        ],
        axis=2,
    )
    region, gate_a = grow_both(packed, gate_a, "gy", 1, (2, 1))
    region, gate_a = grow_both(region, gate_a, "gx", 0, (2, 1))
    size = region.shape[0]
    volume = region[:, :, :flat_z].reshape(size, size, cells_z, channels)
    volume = jnp.pad(volume, ((0, 0), (0, 0), (2, 2), (0, 0)))
    volume = lax.dynamic_slice_in_dim(volume, zside * half, half + 4, axis=2)
    keep = jnp.pad(region[:, :, flat_z : flat_z + cells_z], ((0, 0), (0, 0), (2, 2)))
    keep = lax.dynamic_slice_in_dim(keep, zside * half + 1, half + 2, axis=2)[1:-1, 1:-1]
    activity = convolve(volume, coarse_weight)
    centre = volume[1:-1, 1:-1, 1:-1].astype(jnp.float32)
    hidden = ((centre + jax.nn.silu(activity)) * keep[..., None].astype(jnp.float32)).astype(
        jnp.bfloat16
    )
    cells = hidden.shape[0] * hidden.shape[1]
    hid = jnp.pad(hidden.reshape(cells, -1), ((0, ROWS_C - cells), (0, 0)))

    gate_a = jnp.pad(gate_a, ((0, 0), (0, STRIDE - edge - 2), (0, 0))).reshape(-1, gate_a.shape[2])
    gate_b = jnp.pad(gate_b, ((0, 0), (0, STRIDE - edge), (0, 0))).reshape(-1, width)

    rows = jnp.arange(ROWS_F)
    fx, fy = rows // STRIDE, rows % STRIDE
    inside = (fx < edge + 4) & (fy < edge + 4)
    source = (fx // 2) * (half + 2) + fy // 2
    spread = (inside[:, None] & (source[:, None] == jnp.arange(ROWS_C)[None, :])).astype(
        jnp.bfloat16
    )
    wide = ((0, 0), (0, 1792 - fine_weight_a.shape[1]))
    out = fine_stage(
        hid, spread, gate_a, gate_b, jnp.pad(fine_weight_a, wide), jnp.pad(fine_weight_b, wide)
    )
    return out.reshape(edge, STRIDE, width)[:, :edge]


def solution(mesh):
    in_specs = (
        P(("groups", "gx"), ("gy", "gz"), None),
        P(("groups", "gx"), ("gy", "gz"), None),
        P(("groups", "gx"), "gy", "gz"),
        P(("groups", "gx"), "gy", "gz"),
        P(),
        P(),
        P(),
        P(),
    )
    out_specs = P(("groups", "gx"), "gy", "gz")
    return jax.shard_map(body, mesh=mesh, in_specs=in_specs, out_specs=out_specs, check_vma=False)
```

```python
import jax
import jax.numpy as jnp
from jax import lax
from jax.experimental import pallas as pl
from jax.experimental.pallas import tpu as pltpu
from jax.sharding import PartitionSpec as P

conv_layout = ("NDHWC", "DHWIO", "NDHWC")

STRIDE = 24
ROWS_C = 112
ROWS_F = 488
ROWS_A = 432
ROWS_B = 384
ROWS_L = 440
LANES_F = 1408
LANES_A = 1280
LANES_B = 1024


def select(shape, rule):
    rows = lax.broadcasted_iota(jnp.int32, shape, 0)
    cols = lax.broadcasted_iota(jnp.int32, shape, 1)
    return rule(rows, cols)


def build_bands(w_ref, band_ref):
    rows_all = select((384, 64), lambda r, c: (r & 63) == c).astype(jnp.bfloat16)
    halves = [
        select((128, 256), lambda r, c, h=h: ((r >> 6) == h) & ((r & 63) == (c & 63))).astype(
            jnp.bfloat16
        )
        for h in range(2)
    ]
    for t in range(9):
        acc = jnp.zeros((384, 256), jnp.float32)
        for dz in range(3):
            d = 3 * t + dz
            block = w_ref[:, 128 * (d // 2) : 128 * (d // 2) + 128]
            spread = jnp.dot(block, halves[d % 2], preferred_element_type=jnp.float32)
            tall = jnp.dot(rows_all, spread.astype(jnp.bfloat16), preferred_element_type=jnp.float32)
            keep = select((384, 256), lambda r, c, dz=dz: (r >> 6) - (c >> 6) == dz)
            acc = acc + jnp.where(keep, tall, 0.0)
        band_ref[t] = acc.astype(jnp.bfloat16)


def gate_kernel(field_ref, mw_ref, live_ref, ga_ref, gb_ref):
    tiles = []
    for part in range(2):
        pick = select((128, 128), lambda r, c, p=part: ((r >> 6) == p) & ((r & 63) == (c & 63)))
        spread = jnp.dot(mw_ref[...], pick.astype(jnp.bfloat16), preferred_element_type=jnp.float32)
        rows_all = select((128, 64), lambda r, c: (r & 63) == c).astype(jnp.bfloat16)
        tall = jnp.dot(rows_all, spread.astype(jnp.bfloat16), preferred_element_type=jnp.float32)
        keep = select((128, 128), lambda r, c: (r >> 6) == (c >> 6))
        tiles.append(jnp.where(keep, tall, 0.0).astype(jnp.bfloat16))
    live = live_ref[...]
    for k in range(field_ref.shape[1] // 128):
        lanes = slice(128 * k, 128 * k + 128)
        x = field_ref[:, lanes]
        for tile, out in zip(tiles, (ga_ref, gb_ref)):
            v = jnp.dot(x, tile, preferred_element_type=jnp.float32)
            out[:, lanes] = live / (1.0 + jnp.exp(-v))


def gate_stage(field2d, mod_weight, live_row):
    shape = jax.ShapeDtypeStruct(field2d.shape, jnp.float32)
    return pl.pallas_call(gate_kernel, out_shape=(shape, shape))(field2d, mod_weight, live_row)


def silu(v):
    return v / (1.0 + jnp.exp(-v))


def band_kernel(wa_raw, wb_raw, wa_ref, wb_ref):
    build_bands(wa_raw, wa_ref)
    build_bands(wb_raw, wb_ref)


def band_stage(weight_a, weight_b):
    shape = jax.ShapeDtypeStruct((9, 384, 256), jnp.bfloat16)
    flops = 2 * 27 * 2 * (64 * 128 * 256 + 384 * 64 * 256)
    return pl.pallas_call(
        band_kernel,
        out_shape=(shape, shape),
        cost_estimate=pl.CostEstimate(flops=flops, transcendentals=0, bytes_accessed=4 * 9 * 384 * 256),
    )(weight_a, weight_b)


def fine_kernel(hid_ref, spread_ref, ga_ref, gb_ref, wa_ref, wb_ref, out_ref, fin_ref, lvl_ref):
    wide_c = hid_ref.shape[1]
    i = lax.broadcasted_iota(jnp.int32, (wide_c, LANES_F), 0)
    j = lax.broadcasted_iota(jnp.int32, (wide_c, LANES_F), 1)
    zup = (((i >> 6) == (j >> 7)) & ((i & 63) == (j & 63)) & (j < LANES_A)).astype(jnp.bfloat16)
    deep = jnp.dot(hid_ref[...], zup, preferred_element_type=jnp.float32).astype(jnp.bfloat16)
    fin_ref[...] = jnp.dot(spread_ref[...], deep, preferred_element_type=jnp.float32)
    r = lax.broadcasted_iota(jnp.int32, (384, 256), 0)
    c = lax.broadcasted_iota(jnp.int32, (384, 256), 1)
    shift = (r == c + 64).astype(jnp.bfloat16)
    lvl_ref[ROWS_A:, :] = jnp.zeros((ROWS_L - ROWS_A, LANES_A), jnp.float32)

    def conv(src, weights, rows, chunk):
        acc = jnp.zeros((rows, 256), jnp.float32)
        centre = None
        for t in range(9):
            dx, dy = divmod(t, 3)
            off = dx * STRIDE + dy
            a = src[off : off + rows, 256 * chunk : 256 * chunk + 384].astype(jnp.bfloat16)
            acc = acc + jnp.dot(a, weights[t], preferred_element_type=jnp.float32)
            if t == 4:
                centre = jnp.dot(a, shift, preferred_element_type=jnp.float32)
        return centre, acc

    for k in range(LANES_A // 256):
        centre, acc = conv(fin_ref, wa_ref, ROWS_A, k)
        lanes = slice(256 * k, 256 * k + 256)
        step = centre + silu(acc) * ga_ref[:, lanes]
        lvl_ref[:ROWS_A, lanes] = step.astype(jnp.bfloat16).astype(jnp.float32)
    for k in range(LANES_B // 256):
        centre, acc = conv(lvl_ref, wb_ref, ROWS_B, k)
        lanes = slice(256 * k, 256 * k + 256)
        edge = out_ref.shape[0] // 16
        for x in range(edge):
            mine = slice(x * STRIDE, x * STRIDE + 16)
            value = centre[mine] + silu(acc[mine]) * gb_ref[16 * x : 16 * x + 16, lanes]
            out_ref[16 * x : 16 * x + 16, lanes] = value.astype(out_ref.dtype)


def fine_stage(hid, spread, gate_a, gate_b, band_a, band_b):
    return pl.pallas_call(
        fine_kernel,
        out_shape=jax.ShapeDtypeStruct(gate_b.shape, jnp.bfloat16),
        scratch_shapes=[
            pltpu.VMEM((ROWS_F, LANES_F), jnp.float32),
            pltpu.VMEM((ROWS_L, LANES_A), jnp.float32),
        ],
    )(hid, spread, gate_a, gate_b, band_a, band_b)


def convolve(padded, weight):
    channels = weight.shape[0]
    kernel = weight.reshape(channels, 3, 3, 3, channels).transpose(1, 2, 3, 0, 4)
    result = lax.conv_general_dilated(
        padded[None],
        kernel,
        (1, 1, 1),
        "VALID",
        dimension_numbers=conv_layout,
        preferred_element_type=jnp.float32,
    )
    return result[0]


def shift_pairs(count, up):
    if up:
        return [(k, k + 1) for k in range(count - 1)]
    return [(k + 1, k) for k in range(count - 1)]


def grow_both(cells, gate, axis, dim, widths):
    count = lax.axis_size(axis)
    lanes = gate.shape[-1]

    def ends(arr, width):
        size = arr.shape[dim]
        return lax.slice_in_dim(arr, 0, width, axis=dim), lax.slice_in_dim(arr, size - width, size, axis=dim)

    (cells_head, cells_tail), (gate_head, gate_tail) = ends(cells, widths[0]), ends(gate, widths[1])

    def pack(c, g):
        return jnp.concatenate([c.astype(jnp.float32).reshape(-1, lanes), g.reshape(-1, lanes)], 0)

    def unpack(m):
        split = cells_head.size // lanes
        return m[:split].reshape(cells_head.shape).astype(cells.dtype), m[split:].reshape(gate_head.shape)

    low = unpack(lax.ppermute(pack(cells_tail, gate_tail), axis, shift_pairs(count, True)))
    high = unpack(lax.ppermute(pack(cells_head, gate_head), axis, shift_pairs(count, False)))
    return (
        jnp.concatenate([low[0], cells, high[0]], axis=dim),
        jnp.concatenate([low[1], gate, high[1]], axis=dim),
    )


def grow(cells, axis, dim, width):
    count = lax.axis_size(axis)
    size = cells.shape[dim]
    head = lax.slice_in_dim(cells, 0, width, axis=dim)
    tail = lax.slice_in_dim(cells, size - width, size, axis=dim)
    low = lax.ppermute(tail, axis, shift_pairs(count, True))
    high = lax.ppermute(head, axis, shift_pairs(count, False))
    return jnp.concatenate([low, cells, high], axis=dim)


def body(
    coarse, coarse_mask, brick_live, field, coarse_weight, fine_weight_a, fine_weight_b, mod_weight
):
    channels = coarse_weight.shape[0]
    rows_x, rows_y, flat_z = coarse.shape
    cells_z = flat_z // channels
    edge = field.shape[0]
    half = edge // 2
    assert lax.axis_size("gz") == 2 and rows_x == half and 2 * rows_y == half
    lanes = 256
    zside = lax.axis_index("gz")
    first = zside == 0
    live = brick_live.reshape(())

    extra = jnp.concatenate(
        [
            coarse_mask.astype(jnp.bfloat16),
            jnp.broadcast_to(live.astype(jnp.bfloat16), (rows_x, rows_y, 1)),
            jnp.zeros((rows_x, rows_y, lanes - cells_z - 1), jnp.bfloat16),
        ],
        axis=2,
    )
    mine = jnp.concatenate([coarse, extra], axis=2)
    theirs = lax.ppermute(mine, "gz", [(0, 1), (1, 0)])
    column = jnp.where(first, jnp.concatenate([mine, theirs], 1), jnp.concatenate([theirs, mine], 1))
    live_other = theirs[0, 0, flat_z + cells_z]
    live_mine = live.astype(jnp.bfloat16)
    live_low = jnp.where(first, live_mine, live_other)
    live_high = jnp.where(first, live_other, live_mine)
    zcoarse = lax.broadcasted_iota(jnp.int32, (1, 1, cells_z), 2)
    live_z = jnp.where(zcoarse < half, live_low, live_high)
    keep = column[:, :, flat_z : flat_z + cells_z] * live_z
    packed = jnp.concatenate(
        [
            column[:, :, :flat_z],
            keep,
            jnp.zeros((rows_x, 2 * rows_y, lanes - cells_z), jnp.bfloat16),
        ],
        axis=2,
    )

    live_row = jnp.broadcast_to(live.astype(jnp.float32), (1, 128))
    gate_a, gate_b = gate_stage(field.reshape(edge * edge, -1), mod_weight, live_row)
    gate_a = gate_a.reshape(field.shape)
    width = edge * channels
    face = jnp.where(first, gate_a[:, :, width - channels :], gate_a[:, :, :channels])
    face = lax.ppermute(face, "gz", [(0, 1), (1, 0)])
    blank = jnp.zeros_like(face)
    gate_a = jnp.concatenate(
        [
            jnp.where(first, blank, face),
            gate_a,
            jnp.where(first, face, blank),
            jnp.zeros((edge, edge, 2 * channels), jnp.float32),
        ],
        axis=2,
    )
    region, gate_a = grow_both(packed, gate_a, "gy", 1, (2, 1))
    region, gate_a = grow_both(region, gate_a, "gx", 0, (2, 1))
    size = region.shape[0]
    volume = region[:, :, :flat_z].reshape(size, size, cells_z, channels)
    volume = jnp.pad(volume, ((0, 0), (0, 0), (2, 2), (0, 0)))
    volume = lax.dynamic_slice_in_dim(volume, zside * half, half + 4, axis=2)
    keep = jnp.pad(region[:, :, flat_z : flat_z + cells_z], ((0, 0), (0, 0), (2, 2)))
    keep = lax.dynamic_slice_in_dim(keep, zside * half + 1, half + 2, axis=2)[1:-1, 1:-1]
    activity = convolve(volume, coarse_weight)
    centre = volume[1:-1, 1:-1, 1:-1].astype(jnp.float32)
    hidden = ((centre + jax.nn.silu(activity)) * keep[..., None].astype(jnp.float32)).astype(
        jnp.bfloat16
    )
    cells = hidden.shape[0] * hidden.shape[1]
    hid = jnp.pad(hidden.reshape(cells, -1), ((0, ROWS_C - cells), (0, 0)))

    gate_a = jnp.pad(gate_a, ((0, 0), (0, STRIDE - edge - 2), (0, 0))).reshape(-1, gate_a.shape[2])

    rows = jnp.arange(ROWS_F)
    fx, fy = rows // STRIDE, rows % STRIDE
    inside = (fx < edge + 4) & (fy < edge + 4)
    source = (fx // 2) * (half + 2) + fy // 2
    spread = (inside[:, None] & (source[:, None] == jnp.arange(ROWS_C)[None, :])).astype(
        jnp.bfloat16
    )
    wide = ((0, 0), (0, 1792 - fine_weight_a.shape[1]))
    band_a, band_b = band_stage(jnp.pad(fine_weight_a, wide), jnp.pad(fine_weight_b, wide))
    out = fine_stage(hid, spread, gate_a, gate_b, band_a, band_b)
    return out.reshape(field.shape)


def solution(mesh):
    in_specs = (
        P(("groups", "gx"), ("gy", "gz"), None),
        P(("groups", "gx"), ("gy", "gz"), None),
        P(("groups", "gx"), "gy", "gz"),
        P(("groups", "gx"), "gy", "gz"),
        P(),
        P(),
        P(),
        P(),
    )
    out_specs = P(("groups", "gx"), "gy", "gz")
    return jax.shard_map(body, mesh=mesh, in_specs=in_specs, out_specs=out_specs, check_vma=False)
```

```python
import jax
import jax.numpy as jnp
from jax import lax
from jax.experimental import pallas as pl
from jax.experimental.pallas import tpu as pltpu
from jax.sharding import PartitionSpec as P

conv_layout = ("NDHWC", "DHWIO", "NDHWC")

STRIDE = 24
ROWS_C = 112
ROWS_F = 488
ROWS_A = 432
ROWS_B = 384
ROWS_L = 440
LANES_F = 1408
LANES_A = 1280
LANES_B = 1024


def select(shape, rule):
    rows = lax.broadcasted_iota(jnp.int32, shape, 0)
    cols = lax.broadcasted_iota(jnp.int32, shape, 1)
    return rule(rows, cols)


def build_bands(w_ref, band_ref):
    halves = [
        select((128, 256), lambda r, c, h=h: ((r >> 6) == h) & ((r & 63) == (c & 63))).astype(
            jnp.bfloat16
        )
        for h in range(2)
    ]
    column = select((64, 256), lambda r, c: c >> 6)
    for t in range(9):
        spreads = []
        for dz in range(3):
            d = 3 * t + dz
            block = w_ref[:, 128 * (d // 2) : 128 * (d // 2) + 128]
            spreads.append(jnp.dot(block, halves[d % 2], preferred_element_type=jnp.float32))
        for zi in range(6):
            part = jnp.zeros((64, 256), jnp.float32)
            for dz in range(3):
                part = jnp.where(column == zi - dz, spreads[dz], part)
            band_ref[t, 64 * zi : 64 * zi + 64, :] = part.astype(jnp.bfloat16)


def gate_kernel(field_ref, mw_ref, live_ref, ga_ref, gb_ref):
    tiles = []
    for part in range(2):
        pick = select((128, 128), lambda r, c, p=part: ((r >> 6) == p) & ((r & 63) == (c & 63)))
        spread = jnp.dot(mw_ref[...], pick.astype(jnp.bfloat16), preferred_element_type=jnp.float32)
        rows_all = select((128, 64), lambda r, c: (r & 63) == c).astype(jnp.bfloat16)
        tall = jnp.dot(rows_all, spread.astype(jnp.bfloat16), preferred_element_type=jnp.float32)
        keep = select((128, 128), lambda r, c: (r >> 6) == (c >> 6))
        tiles.append(jnp.where(keep, tall, 0.0).astype(jnp.bfloat16))
    live = live_ref[...]
    for k in range(field_ref.shape[1] // 128):
        lanes = slice(128 * k, 128 * k + 128)
        x = field_ref[:, lanes]
        for tile, out in zip(tiles, (ga_ref, gb_ref)):
            v = jnp.dot(x, tile, preferred_element_type=jnp.float32)
            out[:, lanes] = live / (1.0 + jnp.exp(-v))


def gate_stage(field2d, mod_weight, live_row):
    shape = jax.ShapeDtypeStruct(field2d.shape, jnp.float32)
    return pl.pallas_call(gate_kernel, out_shape=(shape, shape))(field2d, mod_weight, live_row)


def silu(v):
    return v / (1.0 + jnp.exp(-v))


def band_kernel(wa_raw, wb_raw, wa_ref, wb_ref):
    build_bands(wa_raw, wa_ref)
    build_bands(wb_raw, wb_ref)


def band_stage(weight_a, weight_b):
    shape = jax.ShapeDtypeStruct((9, 384, 256), jnp.bfloat16)
    flops = 2 * 27 * 2 * (64 * 128 * 256 + 384 * 64 * 256)
    return pl.pallas_call(
        band_kernel,
        out_shape=(shape, shape),
        cost_estimate=pl.CostEstimate(flops=flops, transcendentals=0, bytes_accessed=4 * 9 * 384 * 256),
    )(weight_a, weight_b)


def fine_kernel(hid_ref, spread_ref, ga_ref, gb_ref, wa_ref, wb_ref, out_ref, fin_ref, lvl_ref):
    wide_c = hid_ref.shape[1]
    i = lax.broadcasted_iota(jnp.int32, (wide_c, LANES_F), 0)
    j = lax.broadcasted_iota(jnp.int32, (wide_c, LANES_F), 1)
    zup = (((i >> 6) == (j >> 7)) & ((i & 63) == (j & 63)) & (j < LANES_A)).astype(jnp.bfloat16)
    deep = jnp.dot(hid_ref[...], zup, preferred_element_type=jnp.float32).astype(jnp.bfloat16)
    fin_ref[...] = jnp.dot(spread_ref[...], deep, preferred_element_type=jnp.float32)
    r = lax.broadcasted_iota(jnp.int32, (384, 256), 0)
    c = lax.broadcasted_iota(jnp.int32, (384, 256), 1)
    shift = (r == c + 64).astype(jnp.bfloat16)
    lvl_ref[ROWS_A:, :] = jnp.zeros((ROWS_L - ROWS_A, LANES_A), jnp.float32)

    def conv(src, weights, rows, chunk):
        acc = jnp.zeros((rows, 256), jnp.float32)
        centre = None
        for t in range(9):
            dx, dy = divmod(t, 3)
            off = dx * STRIDE + dy
            a = src[off : off + rows, 256 * chunk : 256 * chunk + 384].astype(jnp.bfloat16)
            acc = acc + jnp.dot(a, weights[t], preferred_element_type=jnp.float32)
            if t == 4:
                centre = jnp.dot(a, shift, preferred_element_type=jnp.float32)
        return centre, acc

    for k in range(LANES_A // 256):
        centre, acc = conv(fin_ref, wa_ref, ROWS_A, k)
        lanes = slice(256 * k, 256 * k + 256)
        step = centre + silu(acc) * ga_ref[:, lanes]
        lvl_ref[:ROWS_A, lanes] = step.astype(jnp.bfloat16).astype(jnp.float32)
    for k in range(LANES_B // 256):
        centre, acc = conv(lvl_ref, wb_ref, ROWS_B, k)
        lanes = slice(256 * k, 256 * k + 256)
        edge = out_ref.shape[0] // 16
        for x in range(edge):
            mine = slice(x * STRIDE, x * STRIDE + 16)
            value = centre[mine] + silu(acc[mine]) * gb_ref[16 * x : 16 * x + 16, lanes]
            out_ref[16 * x : 16 * x + 16, lanes] = value.astype(out_ref.dtype)


def fine_stage(hid, spread, gate_a, gate_b, band_a, band_b):
    return pl.pallas_call(
        fine_kernel,
        out_shape=jax.ShapeDtypeStruct(gate_b.shape, jnp.bfloat16),
        scratch_shapes=[
            pltpu.VMEM((ROWS_F, LANES_F), jnp.float32),
            pltpu.VMEM((ROWS_L, LANES_A), jnp.float32),
        ],
    )(hid, spread, gate_a, gate_b, band_a, band_b)


def convolve(padded, weight):
    channels = weight.shape[0]
    kernel = weight.reshape(channels, 3, 3, 3, channels).transpose(1, 2, 3, 0, 4)
    result = lax.conv_general_dilated(
        padded[None],
        kernel,
        (1, 1, 1),
        "VALID",
        dimension_numbers=conv_layout,
        preferred_element_type=jnp.float32,
    )
    return result[0]


def shift_pairs(count, up):
    if up:
        return [(k, k + 1) for k in range(count - 1)]
    return [(k + 1, k) for k in range(count - 1)]


def grow_both(cells, gate, axis, dim, widths):
    count = lax.axis_size(axis)
    lanes = gate.shape[-1]

    def ends(arr, width):
        size = arr.shape[dim]
        return lax.slice_in_dim(arr, 0, width, axis=dim), lax.slice_in_dim(arr, size - width, size, axis=dim)

    (cells_head, cells_tail), (gate_head, gate_tail) = ends(cells, widths[0]), ends(gate, widths[1])

    def pack(c, g):
        return jnp.concatenate([c.astype(jnp.float32).reshape(-1, lanes), g.reshape(-1, lanes)], 0)

    def unpack(m):
        split = cells_head.size // lanes
        return m[:split].reshape(cells_head.shape).astype(cells.dtype), m[split:].reshape(gate_head.shape)

    low = unpack(lax.ppermute(pack(cells_tail, gate_tail), axis, shift_pairs(count, True)))
    high = unpack(lax.ppermute(pack(cells_head, gate_head), axis, shift_pairs(count, False)))
    return (
        jnp.concatenate([low[0], cells, high[0]], axis=dim),
        jnp.concatenate([low[1], gate, high[1]], axis=dim),
    )


def grow(cells, axis, dim, width):
    count = lax.axis_size(axis)
    size = cells.shape[dim]
    head = lax.slice_in_dim(cells, 0, width, axis=dim)
    tail = lax.slice_in_dim(cells, size - width, size, axis=dim)
    low = lax.ppermute(tail, axis, shift_pairs(count, True))
    high = lax.ppermute(head, axis, shift_pairs(count, False))
    return jnp.concatenate([low, cells, high], axis=dim)


def body(
    coarse, coarse_mask, brick_live, field, coarse_weight, fine_weight_a, fine_weight_b, mod_weight
):
    channels = coarse_weight.shape[0]
    rows_x, rows_y, flat_z = coarse.shape
    cells_z = flat_z // channels
    edge = field.shape[0]
    half = edge // 2
    assert lax.axis_size("gz") == 2 and rows_x == half and 2 * rows_y == half
    lanes = 256
    zside = lax.axis_index("gz")
    first = zside == 0
    live = brick_live.reshape(())

    extra = jnp.concatenate(
        [
            coarse_mask.astype(jnp.bfloat16),
            jnp.broadcast_to(live.astype(jnp.bfloat16), (rows_x, rows_y, 1)),
            jnp.zeros((rows_x, rows_y, lanes - cells_z - 1), jnp.bfloat16),
        ],
        axis=2,
    )
    mine = jnp.concatenate([coarse, extra], axis=2)
    theirs = lax.ppermute(mine, "gz", [(0, 1), (1, 0)])
    column = jnp.where(first, jnp.concatenate([mine, theirs], 1), jnp.concatenate([theirs, mine], 1))
    live_other = theirs[0, 0, flat_z + cells_z]
    live_mine = live.astype(jnp.bfloat16)
    live_low = jnp.where(first, live_mine, live_other)
    live_high = jnp.where(first, live_other, live_mine)
    zcoarse = lax.broadcasted_iota(jnp.int32, (1, 1, cells_z), 2)
    live_z = jnp.where(zcoarse < half, live_low, live_high)
    keep = column[:, :, flat_z : flat_z + cells_z] * live_z
    packed = jnp.concatenate(
        [
            column[:, :, :flat_z],
            keep,
            jnp.zeros((rows_x, 2 * rows_y, lanes - cells_z), jnp.bfloat16),
        ],
        axis=2,
    )

    live_row = jnp.broadcast_to(live.astype(jnp.float32), (1, 128))
    gate_a, gate_b = gate_stage(field.reshape(edge * edge, -1), mod_weight, live_row)
    gate_a = gate_a.reshape(field.shape)
    width = edge * channels
    face = jnp.where(first, gate_a[:, :, width - channels :], gate_a[:, :, :channels])
    face = lax.ppermute(face, "gz", [(0, 1), (1, 0)])
    blank = jnp.zeros_like(face)
    gate_a = jnp.concatenate(
        [
            jnp.where(first, blank, face),
            gate_a,
            jnp.where(first, face, blank),
            jnp.zeros((edge, edge, 2 * channels), jnp.float32),
        ],
        axis=2,
    )
    region, gate_a = grow_both(packed, gate_a, "gy", 1, (2, 1))
    region, gate_a = grow_both(region, gate_a, "gx", 0, (2, 1))
    size = region.shape[0]
    volume = region[:, :, :flat_z].reshape(size, size, cells_z, channels)
    volume = jnp.pad(volume, ((0, 0), (0, 0), (2, 2), (0, 0)))
    volume = lax.dynamic_slice_in_dim(volume, zside * half, half + 4, axis=2)
    keep = jnp.pad(region[:, :, flat_z : flat_z + cells_z], ((0, 0), (0, 0), (2, 2)))
    keep = lax.dynamic_slice_in_dim(keep, zside * half + 1, half + 2, axis=2)[1:-1, 1:-1]
    activity = convolve(volume, coarse_weight)
    centre = volume[1:-1, 1:-1, 1:-1].astype(jnp.float32)
    hidden = ((centre + jax.nn.silu(activity)) * keep[..., None].astype(jnp.float32)).astype(
        jnp.bfloat16
    )
    cells = hidden.shape[0] * hidden.shape[1]
    hid = jnp.pad(hidden.reshape(cells, -1), ((0, ROWS_C - cells), (0, 0)))

    gate_a = jnp.pad(gate_a, ((0, 0), (0, STRIDE - edge - 2), (0, 0))).reshape(-1, gate_a.shape[2])

    rows = jnp.arange(ROWS_F)
    fx, fy = rows // STRIDE, rows % STRIDE
    inside = (fx < edge + 4) & (fy < edge + 4)
    source = (fx // 2) * (half + 2) + fy // 2
    spread = (inside[:, None] & (source[:, None] == jnp.arange(ROWS_C)[None, :])).astype(
        jnp.bfloat16
    )
    wide = ((0, 0), (0, 1792 - fine_weight_a.shape[1]))
    band_a, band_b = band_stage(jnp.pad(fine_weight_a, wide), jnp.pad(fine_weight_b, wide))
    out = fine_stage(hid, spread, gate_a, gate_b, band_a, band_b)
    return out.reshape(field.shape)


def solution(mesh):
    in_specs = (
        P(("groups", "gx"), ("gy", "gz"), None),
        P(("groups", "gx"), ("gy", "gz"), None),
        P(("groups", "gx"), "gy", "gz"),
        P(("groups", "gx"), "gy", "gz"),
        P(),
        P(),
        P(),
        P(),
    )
    out_specs = P(("groups", "gx"), "gy", "gz")
    return jax.shard_map(body, mesh=mesh, in_specs=in_specs, out_specs=out_specs, check_vma=False)
```

```python
import jax
import jax.numpy as jnp
from jax import lax
from jax.experimental import pallas as pl
from jax.experimental.pallas import tpu as pltpu
from jax.sharding import PartitionSpec as P

conv_layout = ("NDHWC", "DHWIO", "NDHWC")

STRIDE = 24
ROWS_C = 112
ROWS_F = 488
ROWS_A = 432
ROWS_B = 384
ROWS_L = 440
LANES_F = 1408
LANES_A = 1280
LANES_B = 1024


def select(shape, rule):
    rows = lax.broadcasted_iota(jnp.int32, shape, 0)
    cols = lax.broadcasted_iota(jnp.int32, shape, 1)
    return rule(rows, cols)


def build_bands(w_ref, band_ref):
    halves = [
        select((128, 256), lambda r, c, h=h: ((r >> 6) == h) & ((r & 63) == (c & 63))).astype(
            jnp.bfloat16
        )
        for h in range(2)
    ]
    column = select((64, 256), lambda r, c: c >> 6)
    for t in range(9):
        spreads = []
        for dz in range(3):
            d = 3 * t + dz
            block = w_ref[:, 128 * (d // 2) : 128 * (d // 2) + 128]
            spreads.append(jnp.dot(block, halves[d % 2], preferred_element_type=jnp.float32))
        for zi in range(6):
            part = jnp.zeros((64, 256), jnp.float32)
            for dz in range(3):
                part = jnp.where(column == zi - dz, spreads[dz], part)
            band_ref[t, 64 * zi : 64 * zi + 64, :] = part.astype(jnp.bfloat16)


def gate_kernel(field_ref, mw_ref, live_ref, ga_ref, gb_ref):
    tiles = []
    for part in range(2):
        pick = select((128, 128), lambda r, c, p=part: ((r >> 6) == p) & ((r & 63) == (c & 63)))
        spread = jnp.dot(mw_ref[...], pick.astype(jnp.bfloat16), preferred_element_type=jnp.float32)
        rows_all = select((128, 64), lambda r, c: (r & 63) == c).astype(jnp.bfloat16)
        tall = jnp.dot(rows_all, spread.astype(jnp.bfloat16), preferred_element_type=jnp.float32)
        keep = select((128, 128), lambda r, c: (r >> 6) == (c >> 6))
        tiles.append(jnp.where(keep, tall, 0.0).astype(jnp.bfloat16))
    live = live_ref[...]
    for k in range(field_ref.shape[1] // 128):
        lanes = slice(128 * k, 128 * k + 128)
        x = field_ref[:, lanes]
        for tile, out in zip(tiles, (ga_ref, gb_ref)):
            v = jnp.dot(x, tile, preferred_element_type=jnp.float32)
            out[:, lanes] = live / (1.0 + jnp.exp(-v))


def gate_stage(field2d, mod_weight, live_row):
    shape = jax.ShapeDtypeStruct(field2d.shape, jnp.float32)
    return pl.pallas_call(gate_kernel, out_shape=(shape, shape))(field2d, mod_weight, live_row)


def silu(v):
    return v / (1.0 + jnp.exp(-v))


def band_kernel(wa_raw, wb_raw, wa_ref, wb_ref):
    build_bands(wa_raw, wa_ref)
    build_bands(wb_raw, wb_ref)


def band_stage(weight_a, weight_b):
    shape = jax.ShapeDtypeStruct((9, 384, 256), jnp.bfloat16)
    flops = 2 * 27 * 2 * (64 * 128 * 256 + 384 * 64 * 256)
    return pl.pallas_call(
        band_kernel,
        out_shape=(shape, shape),
        cost_estimate=pl.CostEstimate(flops=flops, transcendentals=0, bytes_accessed=4 * 9 * 384 * 256),
    )(weight_a, weight_b)


def fine_kernel(hid_ref, spread_ref, ga_ref, gb_ref, wa_ref, wb_ref, out_ref, fin_ref, lvl_ref):
    wide_c = hid_ref.shape[1]
    i = lax.broadcasted_iota(jnp.int32, (wide_c, LANES_F), 0)
    j = lax.broadcasted_iota(jnp.int32, (wide_c, LANES_F), 1)
    zup = (((i >> 6) == (j >> 7)) & ((i & 63) == (j & 63)) & (j < LANES_A)).astype(jnp.bfloat16)
    deep = jnp.dot(hid_ref[...], zup, preferred_element_type=jnp.float32).astype(jnp.bfloat16)
    fin_ref[...] = jnp.dot(spread_ref[...], deep, preferred_element_type=jnp.float32)
    r = lax.broadcasted_iota(jnp.int32, (384, 256), 0)
    c = lax.broadcasted_iota(jnp.int32, (384, 256), 1)
    shift = (r == c + 64).astype(jnp.bfloat16)
    lvl_ref[ROWS_A:, :] = jnp.zeros((ROWS_L - ROWS_A, LANES_A), jnp.float32)

    def conv(src, weights, rows, chunk):
        acc = jnp.zeros((rows, 256), jnp.float32)
        centre = None
        for t in range(9):
            dx, dy = divmod(t, 3)
            off = dx * STRIDE + dy
            a = src[off : off + rows, 256 * chunk : 256 * chunk + 384].astype(jnp.bfloat16)
            acc = acc + jnp.dot(a, weights[t], preferred_element_type=jnp.float32)
            if t == 4:
                centre = jnp.dot(a, shift, preferred_element_type=jnp.float32)
        return centre, acc

    for k in range(LANES_A // 256):
        centre, acc = conv(fin_ref, wa_ref, ROWS_A, k)
        lanes = slice(256 * k, 256 * k + 256)
        step = centre + silu(acc) * ga_ref[:, lanes]
        lvl_ref[:ROWS_A, lanes] = step.astype(jnp.bfloat16).astype(jnp.float32)
    for k in range(LANES_B // 256):
        centre, acc = conv(lvl_ref, wb_ref, ROWS_B, k)
        lanes = slice(256 * k, 256 * k + 256)
        edge = out_ref.shape[0] // 16
        for x in range(edge):
            mine = slice(x * STRIDE, x * STRIDE + 16)
            value = centre[mine] + silu(acc[mine]) * gb_ref[16 * x : 16 * x + 16, lanes]
            out_ref[16 * x : 16 * x + 16, lanes] = value.astype(out_ref.dtype)


def fine_stage(hid, spread, gate_a, gate_b, band_a, band_b):
    return pl.pallas_call(
        fine_kernel,
        out_shape=jax.ShapeDtypeStruct(gate_b.shape, jnp.bfloat16),
        scratch_shapes=[
            pltpu.VMEM((ROWS_F, LANES_F), jnp.float32),
            pltpu.VMEM((ROWS_L, LANES_A), jnp.float32),
        ],
    )(hid, spread, gate_a, gate_b, band_a, band_b)


def convolve(padded, weight):
    channels = weight.shape[0]
    kernel = weight.reshape(channels, 3, 3, 3, channels).transpose(1, 2, 3, 0, 4)
    result = lax.conv_general_dilated(
        padded[None],
        kernel,
        (1, 1, 1),
        "VALID",
        dimension_numbers=conv_layout,
        preferred_element_type=jnp.float32,
    )
    return result[0]


def shift_pairs(count, up):
    if up:
        return [(k, k + 1) for k in range(count - 1)]
    return [(k + 1, k) for k in range(count - 1)]


def grow_both(cells, gate, axis, dim, widths):
    count = lax.axis_size(axis)
    lanes = gate.shape[-1]

    def ends(arr, width):
        size = arr.shape[dim]
        return lax.slice_in_dim(arr, 0, width, axis=dim), lax.slice_in_dim(arr, size - width, size, axis=dim)

    (cells_head, cells_tail), (gate_head, gate_tail) = ends(cells, widths[0]), ends(gate, widths[1])

    def pack(c, g):
        return jnp.concatenate([c.reshape(-1, lanes), g.astype(c.dtype).reshape(-1, lanes)], 0)

    def unpack(m):
        split = cells_head.size // lanes
        return m[:split].reshape(cells_head.shape), m[split:].reshape(gate_head.shape).astype(gate.dtype)

    low = unpack(lax.ppermute(pack(cells_tail, gate_tail), axis, shift_pairs(count, True)))
    high = unpack(lax.ppermute(pack(cells_head, gate_head), axis, shift_pairs(count, False)))
    return (
        jnp.concatenate([low[0], cells, high[0]], axis=dim),
        jnp.concatenate([low[1], gate, high[1]], axis=dim),
    )


def grow(cells, axis, dim, width):
    count = lax.axis_size(axis)
    size = cells.shape[dim]
    head = lax.slice_in_dim(cells, 0, width, axis=dim)
    tail = lax.slice_in_dim(cells, size - width, size, axis=dim)
    low = lax.ppermute(tail, axis, shift_pairs(count, True))
    high = lax.ppermute(head, axis, shift_pairs(count, False))
    return jnp.concatenate([low, cells, high], axis=dim)


def body(
    coarse, coarse_mask, brick_live, field, coarse_weight, fine_weight_a, fine_weight_b, mod_weight
):
    channels = coarse_weight.shape[0]
    rows_x, rows_y, flat_z = coarse.shape
    cells_z = flat_z // channels
    edge = field.shape[0]
    half = edge // 2
    assert lax.axis_size("gz") == 2 and rows_x == half and 2 * rows_y == half
    lanes = 256
    zside = lax.axis_index("gz")
    first = zside == 0
    live = brick_live.reshape(())

    extra = jnp.concatenate(
        [
            coarse_mask.astype(jnp.bfloat16),
            jnp.broadcast_to(live.astype(jnp.bfloat16), (rows_x, rows_y, 1)),
            jnp.zeros((rows_x, rows_y, lanes - cells_z - 1), jnp.bfloat16),
        ],
        axis=2,
    )
    mine = jnp.concatenate([coarse, extra], axis=2)
    theirs = lax.ppermute(mine, "gz", [(0, 1), (1, 0)])
    column = jnp.where(first, jnp.concatenate([mine, theirs], 1), jnp.concatenate([theirs, mine], 1))
    live_other = theirs[0, 0, flat_z + cells_z]
    live_mine = live.astype(jnp.bfloat16)
    live_low = jnp.where(first, live_mine, live_other)
    live_high = jnp.where(first, live_other, live_mine)
    zcoarse = lax.broadcasted_iota(jnp.int32, (1, 1, cells_z), 2)
    live_z = jnp.where(zcoarse < half, live_low, live_high)
    keep = column[:, :, flat_z : flat_z + cells_z] * live_z
    packed = jnp.concatenate(
        [
            column[:, :, :flat_z],
            keep,
            jnp.zeros((rows_x, 2 * rows_y, lanes - cells_z), jnp.bfloat16),
        ],
        axis=2,
    )

    live_row = jnp.broadcast_to(live.astype(jnp.float32), (1, 128))
    gate_a, gate_b = gate_stage(field.reshape(edge * edge, -1), mod_weight, live_row)
    gate_a = gate_a.reshape(field.shape)
    width = edge * channels
    face = jnp.where(first, gate_a[:, :, width - channels :], gate_a[:, :, :channels])
    face = lax.ppermute(face.astype(jnp.bfloat16), "gz", [(0, 1), (1, 0)]).astype(jnp.float32)
    blank = jnp.zeros_like(face)
    gate_a = jnp.concatenate(
        [
            jnp.where(first, blank, face),
            gate_a,
            jnp.where(first, face, blank),
            jnp.zeros((edge, edge, 2 * channels), jnp.float32),
        ],
        axis=2,
    )
    region, gate_a = grow_both(packed, gate_a, "gy", 1, (2, 1))
    region, gate_a = grow_both(region, gate_a, "gx", 0, (2, 1))
    size = region.shape[0]
    volume = region[:, :, :flat_z].reshape(size, size, cells_z, channels)
    volume = jnp.pad(volume, ((0, 0), (0, 0), (2, 2), (0, 0)))
    volume = lax.dynamic_slice_in_dim(volume, zside * half, half + 4, axis=2)
    keep = jnp.pad(region[:, :, flat_z : flat_z + cells_z], ((0, 0), (0, 0), (2, 2)))
    keep = lax.dynamic_slice_in_dim(keep, zside * half + 1, half + 2, axis=2)[1:-1, 1:-1]
    activity = convolve(volume, coarse_weight)
    centre = volume[1:-1, 1:-1, 1:-1].astype(jnp.float32)
    hidden = ((centre + jax.nn.silu(activity)) * keep[..., None].astype(jnp.float32)).astype(
        jnp.bfloat16
    )
    cells = hidden.shape[0] * hidden.shape[1]
    hid = jnp.pad(hidden.reshape(cells, -1), ((0, ROWS_C - cells), (0, 0)))

    gate_a = jnp.pad(gate_a, ((0, 0), (0, STRIDE - edge - 2), (0, 0))).reshape(-1, gate_a.shape[2])

    rows = jnp.arange(ROWS_F)
    fx, fy = rows // STRIDE, rows % STRIDE
    inside = (fx < edge + 4) & (fy < edge + 4)
    source = (fx // 2) * (half + 2) + fy // 2
    spread = (inside[:, None] & (source[:, None] == jnp.arange(ROWS_C)[None, :])).astype(
        jnp.bfloat16
    )
    wide = ((0, 0), (0, 1792 - fine_weight_a.shape[1]))
    band_a, band_b = band_stage(jnp.pad(fine_weight_a, wide), jnp.pad(fine_weight_b, wide))
    out = fine_stage(hid, spread, gate_a, gate_b, band_a, band_b)
    return out.reshape(field.shape)


def solution(mesh):
    in_specs = (
        P(("groups", "gx"), ("gy", "gz"), None),
        P(("groups", "gx"), ("gy", "gz"), None),
        P(("groups", "gx"), "gy", "gz"),
        P(("groups", "gx"), "gy", "gz"),
        P(),
        P(),
        P(),
        P(),
    )
    out_specs = P(("groups", "gx"), "gy", "gz")
    return jax.shard_map(body, mesh=mesh, in_specs=in_specs, out_specs=out_specs, check_vma=False)
```

```python
import jax
import jax.numpy as jnp
from jax import lax
from jax.experimental import pallas as pl
from jax.experimental.pallas import tpu as pltpu
from jax.sharding import PartitionSpec as P

conv_layout = ("NDHWC", "DHWIO", "NDHWC")

STRIDE = 24
ROWS_C = 112
ROWS_F = 488
ROWS_A = 432
ROWS_B = 384
ROWS_L = 440
LANES_F = 1408
LANES_A = 1280
LANES_B = 1024


def select(shape, rule):
    rows = lax.broadcasted_iota(jnp.int32, shape, 0)
    cols = lax.broadcasted_iota(jnp.int32, shape, 1)
    return rule(rows, cols)


def build_bands(w_ref, band_ref):
    halves = [
        select((128, 256), lambda r, c, h=h: ((r >> 6) == h) & ((r & 63) == (c & 63))).astype(
            jnp.bfloat16
        )
        for h in range(2)
    ]
    column = select((64, 256), lambda r, c: c >> 6)
    for t in range(9):
        spreads = []
        for dz in range(3):
            d = 3 * t + dz
            block = w_ref[:, 128 * (d // 2) : 128 * (d // 2) + 128]
            spreads.append(jnp.dot(block, halves[d % 2], preferred_element_type=jnp.float32))
        for zi in range(6):
            part = jnp.zeros((64, 256), jnp.float32)
            for dz in range(3):
                part = jnp.where(column == zi - dz, spreads[dz], part)
            band_ref[t, 64 * zi : 64 * zi + 64, :] = part.astype(jnp.bfloat16)


def gate_kernel(field_ref, mw_ref, live_ref, ga_ref, gb_ref):
    tiles = []
    for part in range(2):
        pick = select((128, 128), lambda r, c, p=part: ((r >> 6) == p) & ((r & 63) == (c & 63)))
        spread = jnp.dot(mw_ref[...], pick.astype(jnp.bfloat16), preferred_element_type=jnp.float32)
        rows_all = select((128, 64), lambda r, c: (r & 63) == c).astype(jnp.bfloat16)
        tall = jnp.dot(rows_all, spread.astype(jnp.bfloat16), preferred_element_type=jnp.float32)
        keep = select((128, 128), lambda r, c: (r >> 6) == (c >> 6))
        tiles.append(jnp.where(keep, tall, 0.0).astype(jnp.bfloat16))
    live = live_ref[...]
    for k in range(field_ref.shape[1] // 128):
        lanes = slice(128 * k, 128 * k + 128)
        x = field_ref[:, lanes]
        for tile, out in zip(tiles, (ga_ref, gb_ref)):
            v = jnp.dot(x, tile, preferred_element_type=jnp.float32)
            out[:, lanes] = live / (1.0 + jnp.exp(-v))


def gate_stage(field2d, mod_weight, live_row):
    shape = jax.ShapeDtypeStruct(field2d.shape, jnp.float32)
    return pl.pallas_call(gate_kernel, out_shape=(shape, shape))(field2d, mod_weight, live_row)


def silu(v):
    return v / (1.0 + jnp.exp(-v))


def band_kernel(wa_raw, wb_raw, wa_ref, wb_ref):
    build_bands(wa_raw, wa_ref)
    build_bands(wb_raw, wb_ref)


def band_stage(weight_a, weight_b):
    shape = jax.ShapeDtypeStruct((9, 384, 256), jnp.bfloat16)
    flops = 2 * 27 * 2 * (64 * 128 * 256 + 384 * 64 * 256)
    return pl.pallas_call(
        band_kernel,
        out_shape=(shape, shape),
        cost_estimate=pl.CostEstimate(flops=flops, transcendentals=0, bytes_accessed=4 * 9 * 384 * 256),
    )(weight_a, weight_b)


def fine_kernel(hid_ref, spread_ref, ga_ref, gb_ref, wa_ref, wb_ref, out_ref, fin_ref, lvl_ref):
    wide_c = hid_ref.shape[1]
    i = lax.broadcasted_iota(jnp.int32, (wide_c, LANES_F), 0)
    j = lax.broadcasted_iota(jnp.int32, (wide_c, LANES_F), 1)
    zup = (((i >> 6) == (j >> 7)) & ((i & 63) == (j & 63)) & (j < LANES_A)).astype(jnp.bfloat16)
    deep = jnp.dot(hid_ref[...], zup, preferred_element_type=jnp.float32).astype(jnp.bfloat16)
    fin_ref[...] = jnp.dot(spread_ref[...], deep, preferred_element_type=jnp.float32)
    r = lax.broadcasted_iota(jnp.int32, (384, 256), 0)
    c = lax.broadcasted_iota(jnp.int32, (384, 256), 1)
    shift = (r == c + 64).astype(jnp.bfloat16)
    lvl_ref[ROWS_A:, :] = jnp.zeros((ROWS_L - ROWS_A, LANES_A), jnp.float32)

    def conv(src, weights, rows, chunk):
        acc = jnp.zeros((rows, 256), jnp.float32)
        centre = None
        for t in range(9):
            dx, dy = divmod(t, 3)
            off = dx * STRIDE + dy
            a = src[off : off + rows, 256 * chunk : 256 * chunk + 384].astype(jnp.bfloat16)
            acc = acc + jnp.dot(a, weights[t], preferred_element_type=jnp.float32)
            if t == 4:
                centre = jnp.dot(a, shift, preferred_element_type=jnp.float32)
        return centre, acc

    for k in range(LANES_A // 256):
        centre, acc = conv(fin_ref, wa_ref, ROWS_A, k)
        lanes = slice(256 * k, 256 * k + 256)
        step = centre + silu(acc) * ga_ref[:, lanes]
        lvl_ref[:ROWS_A, lanes] = step.astype(jnp.bfloat16).astype(jnp.float32)
    for k in range(LANES_B // 256):
        centre, acc = conv(lvl_ref, wb_ref, ROWS_B, k)
        lanes = slice(256 * k, 256 * k + 256)
        edge = out_ref.shape[0] // 16
        for x in range(edge):
            mine = slice(x * STRIDE, x * STRIDE + 16)
            value = centre[mine] + silu(acc[mine]) * gb_ref[16 * x : 16 * x + 16, lanes]
            out_ref[16 * x : 16 * x + 16, lanes] = value.astype(out_ref.dtype)


def fine_stage(hid, spread, gate_a, gate_b, band_a, band_b):
    return pl.pallas_call(
        fine_kernel,
        out_shape=jax.ShapeDtypeStruct(gate_b.shape, jnp.bfloat16),
        scratch_shapes=[
            pltpu.VMEM((ROWS_F, LANES_F), jnp.float32),
            pltpu.VMEM((ROWS_L, LANES_A), jnp.float32),
        ],
    )(hid, spread, gate_a, gate_b, band_a, band_b)


def convolve(padded, weight):
    channels = weight.shape[0]
    kernel = weight.reshape(channels, 3, 3, 3, channels).transpose(1, 2, 3, 0, 4)
    result = lax.conv_general_dilated(
        padded[None],
        kernel,
        (1, 1, 1),
        "VALID",
        dimension_numbers=conv_layout,
        preferred_element_type=jnp.float32,
    )
    return result[0]


def shift_pairs(count, up):
    if up:
        return [(k, k + 1) for k in range(count - 1)]
    return [(k + 1, k) for k in range(count - 1)]


def grow_both(cells, gate, axis, dim, widths):
    count = lax.axis_size(axis)
    lanes = gate.shape[-1]

    def ends(arr, width):
        size = arr.shape[dim]
        return lax.slice_in_dim(arr, 0, width, axis=dim), lax.slice_in_dim(arr, size - width, size, axis=dim)

    (cells_head, cells_tail), (gate_head, gate_tail) = ends(cells, widths[0]), ends(gate, widths[1])

    def pack(c, g):
        return jnp.concatenate([c.astype(jnp.float32).reshape(-1, lanes), g.reshape(-1, lanes)], 0)

    def unpack(m):
        split = cells_head.size // lanes
        return m[:split].reshape(cells_head.shape).astype(cells.dtype), m[split:].reshape(gate_head.shape)

    low = unpack(lax.ppermute(pack(cells_tail, gate_tail), axis, shift_pairs(count, True)))
    high = unpack(lax.ppermute(pack(cells_head, gate_head), axis, shift_pairs(count, False)))
    return (
        jnp.concatenate([low[0], cells, high[0]], axis=dim),
        jnp.concatenate([low[1], gate, high[1]], axis=dim),
    )


def grow(cells, axis, dim, width):
    count = lax.axis_size(axis)
    size = cells.shape[dim]
    head = lax.slice_in_dim(cells, 0, width, axis=dim)
    tail = lax.slice_in_dim(cells, size - width, size, axis=dim)
    low = lax.ppermute(tail, axis, shift_pairs(count, True))
    high = lax.ppermute(head, axis, shift_pairs(count, False))
    return jnp.concatenate([low, cells, high], axis=dim)


def body(
    coarse, coarse_mask, brick_live, field, coarse_weight, fine_weight_a, fine_weight_b, mod_weight
):
    channels = coarse_weight.shape[0]
    rows_x, rows_y, flat_z = coarse.shape
    cells_z = flat_z // channels
    edge = field.shape[0]
    half = edge // 2
    assert lax.axis_size("gz") == 2 and rows_x == half and 2 * rows_y == half
    lanes = 256
    zside = lax.axis_index("gz")
    first = zside == 0
    live = brick_live.reshape(())

    extra = jnp.concatenate(
        [
            coarse_mask.astype(jnp.bfloat16),
            jnp.broadcast_to(live.astype(jnp.bfloat16), (rows_x, rows_y, 1)),
            jnp.zeros((rows_x, rows_y, lanes - cells_z - 1), jnp.bfloat16),
        ],
        axis=2,
    )
    mine = jnp.concatenate([coarse, extra], axis=2)
    theirs = lax.ppermute(mine, "gz", [(0, 1), (1, 0)])
    column = jnp.where(first, jnp.concatenate([mine, theirs], 1), jnp.concatenate([theirs, mine], 1))
    live_other = theirs[0, 0, flat_z + cells_z]
    live_mine = live.astype(jnp.bfloat16)
    live_low = jnp.where(first, live_mine, live_other)
    live_high = jnp.where(first, live_other, live_mine)
    zcoarse = lax.broadcasted_iota(jnp.int32, (1, 1, cells_z), 2)
    live_z = jnp.where(zcoarse < half, live_low, live_high)
    keep = column[:, :, flat_z : flat_z + cells_z] * live_z
    packed = jnp.concatenate(
        [
            column[:, :, :flat_z],
            keep,
            jnp.zeros((rows_x, 2 * rows_y, lanes - cells_z), jnp.bfloat16),
        ],
        axis=2,
    )

    live_row = jnp.broadcast_to(live.astype(jnp.float32), (1, 128))
    gate_a, gate_b = gate_stage(field.reshape(edge * edge, -1), mod_weight, live_row)
    gate_a = gate_a.reshape(field.shape)
    width = edge * channels
    face = jnp.where(first, gate_a[:, :, width - channels :], gate_a[:, :, :channels])
    face = lax.ppermute(face, "gz", [(0, 1), (1, 0)])
    blank = jnp.zeros_like(face)
    gate_a = jnp.concatenate(
        [
            jnp.where(first, blank, face),
            gate_a,
            jnp.where(first, face, blank),
            jnp.zeros((edge, edge, 2 * channels), jnp.float32),
        ],
        axis=2,
    )
    region, gate_a = grow_both(packed, gate_a, "gy", 1, (2, 1))
    gate_a = jnp.pad(gate_a, ((0, 0), (0, STRIDE - edge - 2), (0, 0)))
    region, gate_a = grow_both(region, gate_a, "gx", 0, (2, 1))
    size = region.shape[0]
    volume = region[:, :, :flat_z].reshape(size, size, cells_z, channels)
    volume = jnp.pad(volume, ((0, 0), (0, 0), (2, 2), (0, 0)))
    volume = lax.dynamic_slice_in_dim(volume, zside * half, half + 4, axis=2)
    keep = jnp.pad(region[:, :, flat_z : flat_z + cells_z], ((0, 0), (0, 0), (2, 2)))
    keep = lax.dynamic_slice_in_dim(keep, zside * half + 1, half + 2, axis=2)[1:-1, 1:-1]
    activity = convolve(volume, coarse_weight)
    centre = volume[1:-1, 1:-1, 1:-1].astype(jnp.float32)
    hidden = ((centre + jax.nn.silu(activity)) * keep[..., None].astype(jnp.float32)).astype(
        jnp.bfloat16
    )
    cells = hidden.shape[0] * hidden.shape[1]
    hid = jnp.pad(hidden.reshape(cells, -1), ((0, ROWS_C - cells), (0, 0)))

    gate_a = gate_a.reshape(-1, gate_a.shape[2])

    rows = jnp.arange(ROWS_F)
    fx, fy = rows // STRIDE, rows % STRIDE
    inside = (fx < edge + 4) & (fy < edge + 4)
    source = (fx // 2) * (half + 2) + fy // 2
    spread = (inside[:, None] & (source[:, None] == jnp.arange(ROWS_C)[None, :])).astype(
        jnp.bfloat16
    )
    wide = ((0, 0), (0, 1792 - fine_weight_a.shape[1]))
    band_a, band_b = band_stage(jnp.pad(fine_weight_a, wide), jnp.pad(fine_weight_b, wide))
    out = fine_stage(hid, spread, gate_a, gate_b, band_a, band_b)
    return out.reshape(field.shape)


def solution(mesh):
    in_specs = (
        P(("groups", "gx"), ("gy", "gz"), None),
        P(("groups", "gx"), ("gy", "gz"), None),
        P(("groups", "gx"), "gy", "gz"),
        P(("groups", "gx"), "gy", "gz"),
        P(),
        P(),
        P(),
        P(),
    )
    out_specs = P(("groups", "gx"), "gy", "gz")
    return jax.shard_map(body, mesh=mesh, in_specs=in_specs, out_specs=out_specs, check_vma=False)
```

```python
import jax
import jax.numpy as jnp
from jax import lax
from jax.experimental import pallas as pl
from jax.experimental.pallas import tpu as pltpu
from jax.sharding import PartitionSpec as P

conv_layout = ("NDHWC", "DHWIO", "NDHWC")

STRIDE = 24
ROWS_C = 112
ROWS_F = 488
ROWS_A = 432
ROWS_B = 384
ROWS_L = 440
LANES_F = 1408
LANES_A = 1280
LANES_B = 1024


def select(shape, rule):
    rows = lax.broadcasted_iota(jnp.int32, shape, 0)
    cols = lax.broadcasted_iota(jnp.int32, shape, 1)
    return rule(rows, cols)


def build_bands(w_ref, band_ref):
    halves = [
        select((128, 256), lambda r, c, h=h: ((r >> 6) == h) & ((r & 63) == (c & 63))).astype(
            jnp.bfloat16
        )
        for h in range(2)
    ]
    column = select((64, 256), lambda r, c: c >> 6)
    for t in range(9):
        spreads = []
        for dz in range(3):
            d = 3 * t + dz
            low = 128 * (d // 2)
            high = min(low + 128, w_ref.shape[1])
            pick = halves[d % 2][: high - low]
            spreads.append(jnp.dot(w_ref[:, low:high], pick, preferred_element_type=jnp.float32))
        for zi in range(6):
            part = jnp.zeros((64, 256), jnp.float32)
            for dz in range(3):
                part = jnp.where(column == zi - dz, spreads[dz], part)
            band_ref[t, 64 * zi : 64 * zi + 64, :] = part.astype(jnp.bfloat16)


def gate_kernel(field_ref, mw_ref, live_ref, ga_ref, gb_ref):
    tiles = []
    for part in range(2):
        pick = select((128, 128), lambda r, c, p=part: ((r >> 6) == p) & ((r & 63) == (c & 63)))
        spread = jnp.dot(mw_ref[...], pick.astype(jnp.bfloat16), preferred_element_type=jnp.float32)
        rows_all = select((128, 64), lambda r, c: (r & 63) == c).astype(jnp.bfloat16)
        tall = jnp.dot(rows_all, spread.astype(jnp.bfloat16), preferred_element_type=jnp.float32)
        keep = select((128, 128), lambda r, c: (r >> 6) == (c >> 6))
        tiles.append(jnp.where(keep, tall, 0.0).astype(jnp.bfloat16))
    live = live_ref[...]
    for k in range(field_ref.shape[1] // 128):
        lanes = slice(128 * k, 128 * k + 128)
        x = field_ref[:, lanes]
        for tile, out in zip(tiles, (ga_ref, gb_ref)):
            v = jnp.dot(x, tile, preferred_element_type=jnp.float32)
            out[:, lanes] = live / (1.0 + jnp.exp(-v))


def gate_stage(field2d, mod_weight, live_row):
    shape = jax.ShapeDtypeStruct(field2d.shape, jnp.float32)
    return pl.pallas_call(gate_kernel, out_shape=(shape, shape))(field2d, mod_weight, live_row)


def silu(v):
    return v / (1.0 + jnp.exp(-v))


def band_kernel(wa_raw, wb_raw, wa_ref, wb_ref):
    build_bands(wa_raw, wa_ref)
    build_bands(wb_raw, wb_ref)


def band_stage(weight_a, weight_b):
    shape = jax.ShapeDtypeStruct((9, 384, 256), jnp.bfloat16)
    flops = 2 * 27 * 2 * (64 * 128 * 256 + 384 * 64 * 256)
    return pl.pallas_call(
        band_kernel,
        out_shape=(shape, shape),
        cost_estimate=pl.CostEstimate(flops=flops, transcendentals=0, bytes_accessed=4 * 9 * 384 * 256),
    )(weight_a, weight_b)


def fine_kernel(hid_ref, spread_ref, ga_ref, gb_ref, wa_ref, wb_ref, out_ref, fin_ref, lvl_ref):
    wide_c = hid_ref.shape[1]
    i = lax.broadcasted_iota(jnp.int32, (wide_c, LANES_F), 0)
    j = lax.broadcasted_iota(jnp.int32, (wide_c, LANES_F), 1)
    zup = (((i >> 6) == (j >> 7)) & ((i & 63) == (j & 63)) & (j < LANES_A)).astype(jnp.bfloat16)
    deep = jnp.dot(hid_ref[...], zup, preferred_element_type=jnp.float32).astype(jnp.bfloat16)
    fin_ref[...] = jnp.dot(spread_ref[...], deep, preferred_element_type=jnp.float32)
    r = lax.broadcasted_iota(jnp.int32, (384, 256), 0)
    c = lax.broadcasted_iota(jnp.int32, (384, 256), 1)
    shift = (r == c + 64).astype(jnp.bfloat16)
    lvl_ref[ROWS_A:, :] = jnp.zeros((ROWS_L - ROWS_A, LANES_A), jnp.float32)

    def conv(src, weights, rows, chunk):
        acc = jnp.zeros((rows, 256), jnp.float32)
        centre = None
        for t in range(9):
            dx, dy = divmod(t, 3)
            off = dx * STRIDE + dy
            a = src[off : off + rows, 256 * chunk : 256 * chunk + 384].astype(jnp.bfloat16)
            acc = acc + jnp.dot(a, weights[t], preferred_element_type=jnp.float32)
            if t == 4:
                centre = jnp.dot(a, shift, preferred_element_type=jnp.float32)
        return centre, acc

    for k in range(LANES_A // 256):
        centre, acc = conv(fin_ref, wa_ref, ROWS_A, k)
        lanes = slice(256 * k, 256 * k + 256)
        step = centre + silu(acc) * ga_ref[:, lanes]
        lvl_ref[:ROWS_A, lanes] = step.astype(jnp.bfloat16).astype(jnp.float32)
    for k in range(LANES_B // 256):
        centre, acc = conv(lvl_ref, wb_ref, ROWS_B, k)
        lanes = slice(256 * k, 256 * k + 256)
        edge = out_ref.shape[0] // 16
        for x in range(edge):
            mine = slice(x * STRIDE, x * STRIDE + 16)
            value = centre[mine] + silu(acc[mine]) * gb_ref[16 * x : 16 * x + 16, lanes]
            out_ref[16 * x : 16 * x + 16, lanes] = value.astype(out_ref.dtype)


def fine_stage(hid, spread, gate_a, gate_b, band_a, band_b):
    return pl.pallas_call(
        fine_kernel,
        out_shape=jax.ShapeDtypeStruct(gate_b.shape, jnp.bfloat16),
        scratch_shapes=[
            pltpu.VMEM((ROWS_F, LANES_F), jnp.float32),
            pltpu.VMEM((ROWS_L, LANES_A), jnp.float32),
        ],
    )(hid, spread, gate_a, gate_b, band_a, band_b)


def convolve(padded, weight):
    channels = weight.shape[0]
    kernel = weight.reshape(channels, 3, 3, 3, channels).transpose(1, 2, 3, 0, 4)
    result = lax.conv_general_dilated(
        padded[None],
        kernel,
        (1, 1, 1),
        "VALID",
        dimension_numbers=conv_layout,
        preferred_element_type=jnp.float32,
    )
    return result[0]


def shift_pairs(count, up):
    if up:
        return [(k, k + 1) for k in range(count - 1)]
    return [(k + 1, k) for k in range(count - 1)]


def grow_both(cells, gate, axis, dim, widths):
    count = lax.axis_size(axis)
    lanes = gate.shape[-1]

    def ends(arr, width):
        size = arr.shape[dim]
        return lax.slice_in_dim(arr, 0, width, axis=dim), lax.slice_in_dim(arr, size - width, size, axis=dim)

    (cells_head, cells_tail), (gate_head, gate_tail) = ends(cells, widths[0]), ends(gate, widths[1])

    def pack(c, g):
        return jnp.concatenate([c.astype(jnp.float32).reshape(-1, lanes), g.reshape(-1, lanes)], 0)

    def unpack(m):
        split = cells_head.size // lanes
        return m[:split].reshape(cells_head.shape).astype(cells.dtype), m[split:].reshape(gate_head.shape)

    low = unpack(lax.ppermute(pack(cells_tail, gate_tail), axis, shift_pairs(count, True)))
    high = unpack(lax.ppermute(pack(cells_head, gate_head), axis, shift_pairs(count, False)))
    return (
        jnp.concatenate([low[0], cells, high[0]], axis=dim),
        jnp.concatenate([low[1], gate, high[1]], axis=dim),
    )


def grow(cells, axis, dim, width):
    count = lax.axis_size(axis)
    size = cells.shape[dim]
    head = lax.slice_in_dim(cells, 0, width, axis=dim)
    tail = lax.slice_in_dim(cells, size - width, size, axis=dim)
    low = lax.ppermute(tail, axis, shift_pairs(count, True))
    high = lax.ppermute(head, axis, shift_pairs(count, False))
    return jnp.concatenate([low, cells, high], axis=dim)


def body(
    coarse, coarse_mask, brick_live, field, coarse_weight, fine_weight_a, fine_weight_b, mod_weight
):
    channels = coarse_weight.shape[0]
    rows_x, rows_y, flat_z = coarse.shape
    cells_z = flat_z // channels
    edge = field.shape[0]
    half = edge // 2
    assert lax.axis_size("gz") == 2 and rows_x == half and 2 * rows_y == half
    lanes = 256
    zside = lax.axis_index("gz")
    first = zside == 0
    live = brick_live.reshape(())

    extra = jnp.concatenate(
        [
            coarse_mask.astype(jnp.bfloat16),
            jnp.broadcast_to(live.astype(jnp.bfloat16), (rows_x, rows_y, 1)),
            jnp.zeros((rows_x, rows_y, lanes - cells_z - 1), jnp.bfloat16),
        ],
        axis=2,
    )
    mine = jnp.concatenate([coarse, extra], axis=2)
    theirs = lax.ppermute(mine, "gz", [(0, 1), (1, 0)])
    column = jnp.where(first, jnp.concatenate([mine, theirs], 1), jnp.concatenate([theirs, mine], 1))
    live_other = theirs[0, 0, flat_z + cells_z]
    live_mine = live.astype(jnp.bfloat16)
    live_low = jnp.where(first, live_mine, live_other)
    live_high = jnp.where(first, live_other, live_mine)
    zcoarse = lax.broadcasted_iota(jnp.int32, (1, 1, cells_z), 2)
    live_z = jnp.where(zcoarse < half, live_low, live_high)
    keep = column[:, :, flat_z : flat_z + cells_z] * live_z
    packed = jnp.concatenate(
        [
            column[:, :, :flat_z],
            keep,
            jnp.zeros((rows_x, 2 * rows_y, lanes - cells_z), jnp.bfloat16),
        ],
        axis=2,
    )

    live_row = jnp.broadcast_to(live.astype(jnp.float32), (1, 128))
    gate_a, gate_b = gate_stage(field.reshape(edge * edge, -1), mod_weight, live_row)
    gate_a = gate_a.reshape(field.shape)
    width = edge * channels
    face = jnp.where(first, gate_a[:, :, width - channels :], gate_a[:, :, :channels])
    face = lax.ppermute(face, "gz", [(0, 1), (1, 0)])
    blank = jnp.zeros_like(face)
    gate_a = jnp.concatenate(
        [
            jnp.where(first, blank, face),
            gate_a,
            jnp.where(first, face, blank),
            jnp.zeros((edge, edge, 2 * channels), jnp.float32),
        ],
        axis=2,
    )
    region, gate_a = grow_both(packed, gate_a, "gy", 1, (2, 1))
    region, gate_a = grow_both(region, gate_a, "gx", 0, (2, 1))
    size = region.shape[0]
    volume = region[:, :, :flat_z].reshape(size, size, cells_z, channels)
    volume = jnp.pad(volume, ((0, 0), (0, 0), (2, 2), (0, 0)))
    volume = lax.dynamic_slice_in_dim(volume, zside * half, half + 4, axis=2)
    keep = jnp.pad(region[:, :, flat_z : flat_z + cells_z], ((0, 0), (0, 0), (2, 2)))
    keep = lax.dynamic_slice_in_dim(keep, zside * half + 1, half + 2, axis=2)[1:-1, 1:-1]
    activity = convolve(volume, coarse_weight)
    centre = volume[1:-1, 1:-1, 1:-1].astype(jnp.float32)
    hidden = ((centre + jax.nn.silu(activity)) * keep[..., None].astype(jnp.float32)).astype(
        jnp.bfloat16
    )
    cells = hidden.shape[0] * hidden.shape[1]
    hid = jnp.pad(hidden.reshape(cells, -1), ((0, ROWS_C - cells), (0, 0)))

    gate_a = jnp.pad(gate_a, ((0, 0), (0, STRIDE - edge - 2), (0, 0))).reshape(-1, gate_a.shape[2])

    rows = jnp.arange(ROWS_F)
    fx, fy = rows // STRIDE, rows % STRIDE
    inside = (fx < edge + 4) & (fy < edge + 4)
    source = (fx // 2) * (half + 2) + fy // 2
    spread = (inside[:, None] & (source[:, None] == jnp.arange(ROWS_C)[None, :])).astype(
        jnp.bfloat16
    )
    band_a, band_b = band_stage(fine_weight_a, fine_weight_b)
    out = fine_stage(hid, spread, gate_a, gate_b, band_a, band_b)
    return out.reshape(field.shape)


def solution(mesh):
    in_specs = (
        P(("groups", "gx"), ("gy", "gz"), None),
        P(("groups", "gx"), ("gy", "gz"), None),
        P(("groups", "gx"), "gy", "gz"),
        P(("groups", "gx"), "gy", "gz"),
        P(),
        P(),
        P(),
        P(),
    )
    out_specs = P(("groups", "gx"), "gy", "gz")
    return jax.shard_map(body, mesh=mesh, in_specs=in_specs, out_specs=out_specs, check_vma=False)
```

```python
import jax
import jax.numpy as jnp
from jax import lax
from jax.experimental import pallas as pl
from jax.experimental.pallas import tpu as pltpu
from jax.sharding import PartitionSpec as P

conv_layout = ("NDHWC", "DHWIO", "NDHWC")

STRIDE = 24
ROWS_C = 112
ROWS_F = 488
ROWS_A = 432
ROWS_B = 384
ROWS_L = 440
LANES_F = 1408
LANES_A = 1280
LANES_B = 1024


def select(shape, rule):
    rows = lax.broadcasted_iota(jnp.int32, shape, 0)
    cols = lax.broadcasted_iota(jnp.int32, shape, 1)
    return rule(rows, cols)


def build_bands(w_ref, band_ref):
    halves = [
        select((128, 256), lambda r, c, h=h: ((r >> 6) == h) & ((r & 63) == (c & 63))).astype(
            jnp.bfloat16
        )
        for h in range(2)
    ]
    column = select((64, 256), lambda r, c: c >> 6)
    for t in range(9):
        spreads = []
        for dz in range(3):
            d = 3 * t + dz
            low = 128 * (d // 2)
            high = min(low + 128, w_ref.shape[1])
            pick = halves[d % 2][: high - low]
            spreads.append(jnp.dot(w_ref[:, low:high], pick, preferred_element_type=jnp.float32))
        for zi in range(6):
            part = jnp.zeros((64, 256), jnp.float32)
            for dz in range(3):
                part = jnp.where(column == zi - dz, spreads[dz], part)
            band_ref[t, 64 * zi : 64 * zi + 64, :] = part.astype(jnp.bfloat16)


def gate_kernel(field_ref, mw_ref, live_ref, ga_ref, gb_ref):
    tiles = []
    for part in range(2):
        pick = select((128, 128), lambda r, c, p=part: ((r >> 6) == p) & ((r & 63) == (c & 63)))
        spread = jnp.dot(mw_ref[...], pick.astype(jnp.bfloat16), preferred_element_type=jnp.float32)
        rows_all = select((128, 64), lambda r, c: (r & 63) == c).astype(jnp.bfloat16)
        tall = jnp.dot(rows_all, spread.astype(jnp.bfloat16), preferred_element_type=jnp.float32)
        keep = select((128, 128), lambda r, c: (r >> 6) == (c >> 6))
        tiles.append(jnp.where(keep, tall, 0.0).astype(jnp.bfloat16))
    live = live_ref[...]
    for k in range(field_ref.shape[1] // 128):
        lanes = slice(128 * k, 128 * k + 128)
        x = field_ref[:, lanes]
        for tile, out in zip(tiles, (ga_ref, gb_ref)):
            v = jnp.dot(x, tile, preferred_element_type=jnp.float32)
            out[:, lanes] = live / (1.0 + jnp.exp(-v))


def gate_stage(field2d, mod_weight, live_row):
    shape = jax.ShapeDtypeStruct(field2d.shape, jnp.float32)
    return pl.pallas_call(gate_kernel, out_shape=(shape, shape))(field2d, mod_weight, live_row)


def silu(v):
    return v / (1.0 + jnp.exp(-v))


def band_kernel(wa_raw, wb_raw, wa_ref, wb_ref):
    build_bands(wa_raw, wa_ref)
    build_bands(wb_raw, wb_ref)


def band_stage(weight_a, weight_b):
    shape = jax.ShapeDtypeStruct((9, 384, 256), jnp.bfloat16)
    flops = 2 * 27 * 2 * (64 * 128 * 256 + 384 * 64 * 256)
    return pl.pallas_call(
        band_kernel,
        out_shape=(shape, shape),
        cost_estimate=pl.CostEstimate(flops=flops, transcendentals=0, bytes_accessed=4 * 9 * 384 * 256),
    )(weight_a, weight_b)


def fine_kernel(
    hid_ref, spread_ref, core_ref, yl_ref, yh_ref, xl_ref, xh_ref, gb_ref, wa_ref, wb_ref,
    out_ref, fin_ref, lvl_ref, ga_ref,
):
    edge = core_ref.shape[0] // 16
    ga_ref[...] = jnp.zeros(ga_ref.shape, jnp.float32)
    for x in range(edge):
        base = (x + 1) * STRIDE
        ga_ref[base + 1 : base + 1 + edge, :] = core_ref[edge * x : edge * x + edge, :]
        ga_ref[base : base + 1, :] = yl_ref[x : x + 1, :]
        ga_ref[base + edge + 1 : base + edge + 2, :] = yh_ref[x : x + 1, :]
    ga_ref[: edge + 2, :] = xl_ref[...]
    ga_ref[(edge + 1) * STRIDE : (edge + 1) * STRIDE + edge + 2, :] = xh_ref[...]
    wide_c = hid_ref.shape[1]
    i = lax.broadcasted_iota(jnp.int32, (wide_c, LANES_F), 0)
    j = lax.broadcasted_iota(jnp.int32, (wide_c, LANES_F), 1)
    zup = (((i >> 6) == (j >> 7)) & ((i & 63) == (j & 63)) & (j < LANES_A)).astype(jnp.bfloat16)
    deep = jnp.dot(hid_ref[...], zup, preferred_element_type=jnp.float32).astype(jnp.bfloat16)
    fin_ref[...] = jnp.dot(spread_ref[...], deep, preferred_element_type=jnp.float32)
    r = lax.broadcasted_iota(jnp.int32, (384, 256), 0)
    c = lax.broadcasted_iota(jnp.int32, (384, 256), 1)
    shift = (r == c + 64).astype(jnp.bfloat16)
    lvl_ref[ROWS_A:, :] = jnp.zeros((ROWS_L - ROWS_A, LANES_A), jnp.float32)

    def conv(src, weights, rows, chunk):
        acc = jnp.zeros((rows, 256), jnp.float32)
        centre = None
        for t in range(9):
            dx, dy = divmod(t, 3)
            off = dx * STRIDE + dy
            a = src[off : off + rows, 256 * chunk : 256 * chunk + 384].astype(jnp.bfloat16)
            acc = acc + jnp.dot(a, weights[t], preferred_element_type=jnp.float32)
            if t == 4:
                centre = jnp.dot(a, shift, preferred_element_type=jnp.float32)
        return centre, acc

    for k in range(LANES_A // 256):
        centre, acc = conv(fin_ref, wa_ref, ROWS_A, k)
        lanes = slice(256 * k, 256 * k + 256)
        step = centre + silu(acc) * ga_ref[:, lanes]
        lvl_ref[:ROWS_A, lanes] = step.astype(jnp.bfloat16).astype(jnp.float32)
    for k in range(LANES_B // 256):
        centre, acc = conv(lvl_ref, wb_ref, ROWS_B, k)
        lanes = slice(256 * k, 256 * k + 256)
        for x in range(edge):
            mine = slice(x * STRIDE, x * STRIDE + 16)
            value = centre[mine] + silu(acc[mine]) * gb_ref[16 * x : 16 * x + 16, lanes]
            out_ref[16 * x : 16 * x + 16, lanes] = value.astype(out_ref.dtype)


def fine_stage(hid, spread, gate_parts, gate_b, band_a, band_b):
    return pl.pallas_call(
        fine_kernel,
        out_shape=jax.ShapeDtypeStruct(gate_b.shape, jnp.bfloat16),
        scratch_shapes=[
            pltpu.VMEM((ROWS_F, LANES_F), jnp.float32),
            pltpu.VMEM((ROWS_L, LANES_A), jnp.float32),
            pltpu.VMEM((ROWS_A, LANES_A), jnp.float32),
        ],
    )(hid, spread, *gate_parts, gate_b, band_a, band_b)


def convolve(padded, weight):
    channels = weight.shape[0]
    kernel = weight.reshape(channels, 3, 3, 3, channels).transpose(1, 2, 3, 0, 4)
    result = lax.conv_general_dilated(
        padded[None],
        kernel,
        (1, 1, 1),
        "VALID",
        dimension_numbers=conv_layout,
        preferred_element_type=jnp.float32,
    )
    return result[0]


def shift_pairs(count, up):
    if up:
        return [(k, k + 1) for k in range(count - 1)]
    return [(k + 1, k) for k in range(count - 1)]


def grow_both(cells, gate_head, gate_tail, axis, dim, width):
    count = lax.axis_size(axis)
    lanes = gate_head.shape[-1]
    size = cells.shape[dim]
    cells_head = lax.slice_in_dim(cells, 0, width, axis=dim)
    cells_tail = lax.slice_in_dim(cells, size - width, size, axis=dim)

    def pack(c, g):
        return jnp.concatenate([c.astype(jnp.float32).reshape(-1, lanes), g.reshape(-1, lanes)], 0)

    def unpack(m):
        split = cells_head.size // lanes
        return m[:split].reshape(cells_head.shape).astype(cells.dtype), m[split:].reshape(gate_head.shape)

    low = unpack(lax.ppermute(pack(cells_tail, gate_tail), axis, shift_pairs(count, True)))
    high = unpack(lax.ppermute(pack(cells_head, gate_head), axis, shift_pairs(count, False)))
    return jnp.concatenate([low[0], cells, high[0]], axis=dim), low[1], high[1]


def grow(cells, axis, dim, width):
    count = lax.axis_size(axis)
    size = cells.shape[dim]
    head = lax.slice_in_dim(cells, 0, width, axis=dim)
    tail = lax.slice_in_dim(cells, size - width, size, axis=dim)
    low = lax.ppermute(tail, axis, shift_pairs(count, True))
    high = lax.ppermute(head, axis, shift_pairs(count, False))
    return jnp.concatenate([low, cells, high], axis=dim)


def body(
    coarse, coarse_mask, brick_live, field, coarse_weight, fine_weight_a, fine_weight_b, mod_weight
):
    channels = coarse_weight.shape[0]
    rows_x, rows_y, flat_z = coarse.shape
    cells_z = flat_z // channels
    edge = field.shape[0]
    half = edge // 2
    assert lax.axis_size("gz") == 2 and rows_x == half and 2 * rows_y == half
    lanes = 256
    zside = lax.axis_index("gz")
    first = zside == 0
    live = brick_live.reshape(())

    extra = jnp.concatenate(
        [
            coarse_mask.astype(jnp.bfloat16),
            jnp.broadcast_to(live.astype(jnp.bfloat16), (rows_x, rows_y, 1)),
            jnp.zeros((rows_x, rows_y, lanes - cells_z - 1), jnp.bfloat16),
        ],
        axis=2,
    )
    mine = jnp.concatenate([coarse, extra], axis=2)
    theirs = lax.ppermute(mine, "gz", [(0, 1), (1, 0)])
    column = jnp.where(first, jnp.concatenate([mine, theirs], 1), jnp.concatenate([theirs, mine], 1))
    live_other = theirs[0, 0, flat_z + cells_z]
    live_mine = live.astype(jnp.bfloat16)
    live_low = jnp.where(first, live_mine, live_other)
    live_high = jnp.where(first, live_other, live_mine)
    zcoarse = lax.broadcasted_iota(jnp.int32, (1, 1, cells_z), 2)
    live_z = jnp.where(zcoarse < half, live_low, live_high)
    keep = column[:, :, flat_z : flat_z + cells_z] * live_z
    packed = jnp.concatenate(
        [
            column[:, :, :flat_z],
            keep,
            jnp.zeros((rows_x, 2 * rows_y, lanes - cells_z), jnp.bfloat16),
        ],
        axis=2,
    )

    live_row = jnp.broadcast_to(live.astype(jnp.float32), (1, 128))
    gate_a, gate_b = gate_stage(field.reshape(edge * edge, -1), mod_weight, live_row)
    gate_a = gate_a.reshape(field.shape)
    width = edge * channels
    face = jnp.where(first, gate_a[:, :, width - channels :], gate_a[:, :, :channels])
    face = lax.ppermute(face, "gz", [(0, 1), (1, 0)])
    blank = jnp.zeros_like(face)
    gate_a = jnp.concatenate(
        [
            jnp.where(first, blank, face),
            gate_a,
            jnp.where(first, face, blank),
            jnp.zeros((edge, edge, 2 * channels), jnp.float32),
        ],
        axis=2,
    )
    region, side_low, side_high = grow_both(packed, gate_a[:, 0], gate_a[:, -1], "gy", 1, 2)
    planes = [
        jnp.concatenate([side_low[x : x + 1], gate_a[x], side_high[x : x + 1]], 0) for x in (0, edge - 1)
    ]
    region, end_low, end_high = grow_both(region, planes[0], planes[1], "gx", 0, 2)
    gate_parts = (gate_a.reshape(edge * edge, -1), side_low, side_high, end_low, end_high)
    size = region.shape[0]
    volume = region[:, :, :flat_z].reshape(size, size, cells_z, channels)
    volume = jnp.pad(volume, ((0, 0), (0, 0), (2, 2), (0, 0)))
    volume = lax.dynamic_slice_in_dim(volume, zside * half, half + 4, axis=2)
    keep = jnp.pad(region[:, :, flat_z : flat_z + cells_z], ((0, 0), (0, 0), (2, 2)))
    keep = lax.dynamic_slice_in_dim(keep, zside * half + 1, half + 2, axis=2)[1:-1, 1:-1]
    activity = convolve(volume, coarse_weight)
    centre = volume[1:-1, 1:-1, 1:-1].astype(jnp.float32)
    hidden = ((centre + jax.nn.silu(activity)) * keep[..., None].astype(jnp.float32)).astype(
        jnp.bfloat16
    )
    cells = hidden.shape[0] * hidden.shape[1]
    hid = jnp.pad(hidden.reshape(cells, -1), ((0, ROWS_C - cells), (0, 0)))


    rows = jnp.arange(ROWS_F)
    fx, fy = rows // STRIDE, rows % STRIDE
    inside = (fx < edge + 4) & (fy < edge + 4)
    source = (fx // 2) * (half + 2) + fy // 2
    spread = (inside[:, None] & (source[:, None] == jnp.arange(ROWS_C)[None, :])).astype(
        jnp.bfloat16
    )
    band_a, band_b = band_stage(fine_weight_a, fine_weight_b)
    out = fine_stage(hid, spread, gate_parts, gate_b, band_a, band_b)
    return out.reshape(field.shape)


def solution(mesh):
    in_specs = (
        P(("groups", "gx"), ("gy", "gz"), None),
        P(("groups", "gx"), ("gy", "gz"), None),
        P(("groups", "gx"), "gy", "gz"),
        P(("groups", "gx"), "gy", "gz"),
        P(),
        P(),
        P(),
        P(),
    )
    out_specs = P(("groups", "gx"), "gy", "gz")
    return jax.shard_map(body, mesh=mesh, in_specs=in_specs, out_specs=out_specs, check_vma=False)
```

```python
import jax
import jax.numpy as jnp
from jax import lax
from jax.experimental import pallas as pl
from jax.experimental.pallas import tpu as pltpu
from jax.sharding import PartitionSpec as P

conv_layout = ("NDHWC", "DHWIO", "NDHWC")

STRIDE = 24
ROWS_C = 112
ROWS_F = 488
ROWS_A = 432
ROWS_B = 384
ROWS_L = 440
LANES_F = 1408
LANES_A = 1280
LANES_B = 1024


def select(shape, rule):
    rows = lax.broadcasted_iota(jnp.int32, shape, 0)
    cols = lax.broadcasted_iota(jnp.int32, shape, 1)
    return rule(rows, cols)


def build_bands(w_ref, band_ref):
    halves = [
        select((128, 256), lambda r, c, h=h: ((r >> 6) == h) & ((r & 63) == (c & 63))).astype(
            jnp.bfloat16
        )
        for h in range(2)
    ]
    column = select((64, 256), lambda r, c: c >> 6)
    for t in range(9):
        spreads = []
        for dz in range(3):
            d = 3 * t + dz
            low = 128 * (d // 2)
            high = min(low + 128, w_ref.shape[1])
            pick = halves[d % 2][: high - low]
            spreads.append(jnp.dot(w_ref[:, low:high], pick, preferred_element_type=jnp.float32))
        for zi in range(6):
            part = jnp.zeros((64, 256), jnp.float32)
            for dz in range(3):
                part = jnp.where(column == zi - dz, spreads[dz], part)
            band_ref[t, 64 * zi : 64 * zi + 64, :] = part.astype(jnp.bfloat16)


def gate_kernel(field_ref, mw_ref, live_ref, ga_ref, gb_ref):
    tiles = []
    for part in range(2):
        pick = select((128, 128), lambda r, c, p=part: ((r >> 6) == p) & ((r & 63) == (c & 63)))
        spread = jnp.dot(mw_ref[...], pick.astype(jnp.bfloat16), preferred_element_type=jnp.float32)
        rows_all = select((128, 64), lambda r, c: (r & 63) == c).astype(jnp.bfloat16)
        tall = jnp.dot(rows_all, spread.astype(jnp.bfloat16), preferred_element_type=jnp.float32)
        keep = select((128, 128), lambda r, c: (r >> 6) == (c >> 6))
        tiles.append(jnp.where(keep, tall, 0.0).astype(jnp.bfloat16))
    live = live_ref[...]
    swap = select((256, 256), lambda r, c: c == (r & 15) * 16 + (r >> 4)).astype(jnp.bfloat16)
    swapped = jnp.dot(swap, field_ref[...], preferred_element_type=jnp.float32).astype(jnp.bfloat16)
    for k in range(field_ref.shape[1] // 128):
        lanes = slice(128 * k, 128 * k + 128)
        for tile, out, x in zip(tiles, (ga_ref, gb_ref), (swapped[:, lanes], field_ref[:, lanes])):
            v = jnp.dot(x, tile, preferred_element_type=jnp.float32)
            out[:, lanes] = live / (1.0 + jnp.exp(-v))


def gate_stage(field2d, mod_weight, live_row):
    shape = jax.ShapeDtypeStruct(field2d.shape, jnp.float32)
    return pl.pallas_call(gate_kernel, out_shape=(shape, shape))(field2d, mod_weight, live_row)


def silu(v):
    return v / (1.0 + jnp.exp(-v))


def band_kernel(wa_raw, wb_raw, wa_ref, wb_ref):
    build_bands(wa_raw, wa_ref)
    build_bands(wb_raw, wb_ref)


def band_stage(weight_a, weight_b):
    shape = jax.ShapeDtypeStruct((9, 384, 256), jnp.bfloat16)
    flops = 2 * 27 * 2 * (64 * 128 * 256 + 384 * 64 * 256)
    return pl.pallas_call(
        band_kernel,
        out_shape=(shape, shape),
        cost_estimate=pl.CostEstimate(flops=flops, transcendentals=0, bytes_accessed=4 * 9 * 384 * 256),
    )(weight_a, weight_b)


def fine_kernel(hid_ref, spread_ref, ga_ref, gb_ref, wa_ref, wb_ref, out_ref, fin_ref, lvl_ref):
    wide_c = hid_ref.shape[1]
    i = lax.broadcasted_iota(jnp.int32, (wide_c, LANES_F), 0)
    j = lax.broadcasted_iota(jnp.int32, (wide_c, LANES_F), 1)
    zup = (((i >> 6) == (j >> 7)) & ((i & 63) == (j & 63)) & (j < LANES_A)).astype(jnp.bfloat16)
    deep = jnp.dot(hid_ref[...], zup, preferred_element_type=jnp.float32).astype(jnp.bfloat16)
    fin_ref[...] = jnp.dot(spread_ref[...], deep, preferred_element_type=jnp.float32)
    r = lax.broadcasted_iota(jnp.int32, (384, 256), 0)
    c = lax.broadcasted_iota(jnp.int32, (384, 256), 1)
    shift = (r == c + 64).astype(jnp.bfloat16)
    lvl_ref[ROWS_A:, :] = jnp.zeros((ROWS_L - ROWS_A, LANES_A), jnp.float32)

    def conv(src, weights, rows, chunk):
        acc = jnp.zeros((rows, 256), jnp.float32)
        centre = None
        for t in range(9):
            dx, dy = divmod(t, 3)
            off = dx * STRIDE + dy
            a = src[off : off + rows, 256 * chunk : 256 * chunk + 384].astype(jnp.bfloat16)
            acc = acc + jnp.dot(a, weights[t], preferred_element_type=jnp.float32)
            if t == 4:
                centre = jnp.dot(a, shift, preferred_element_type=jnp.float32)
        return centre, acc

    for k in range(LANES_A // 256):
        centre, acc = conv(fin_ref, wa_ref, ROWS_A, k)
        lanes = slice(256 * k, 256 * k + 256)
        step = centre + silu(acc) * ga_ref[:, lanes]
        lvl_ref[:ROWS_A, lanes] = step.astype(jnp.bfloat16).astype(jnp.float32)
    for k in range(LANES_B // 256):
        centre, acc = conv(lvl_ref, wb_ref, ROWS_B, k)
        lanes = slice(256 * k, 256 * k + 256)
        edge = out_ref.shape[0] // 16
        for x in range(edge):
            mine = slice(x * STRIDE, x * STRIDE + 16)
            value = centre[mine] + silu(acc[mine]) * gb_ref[16 * x : 16 * x + 16, lanes]
            out_ref[16 * x : 16 * x + 16, lanes] = value.astype(out_ref.dtype)


def fine_stage(hid, spread, gate_a, gate_b, band_a, band_b):
    return pl.pallas_call(
        fine_kernel,
        out_shape=jax.ShapeDtypeStruct(gate_b.shape, jnp.bfloat16),
        scratch_shapes=[
            pltpu.VMEM((ROWS_F, LANES_F), jnp.float32),
            pltpu.VMEM((ROWS_L, LANES_A), jnp.float32),
        ],
    )(hid, spread, gate_a, gate_b, band_a, band_b)


def convolve(padded, weight):
    channels = weight.shape[0]
    kernel = weight.reshape(channels, 3, 3, 3, channels).transpose(1, 2, 3, 0, 4)
    result = lax.conv_general_dilated(
        padded[None],
        kernel,
        (1, 1, 1),
        "VALID",
        dimension_numbers=conv_layout,
        preferred_element_type=jnp.float32,
    )
    return result[0]


def shift_pairs(count, up):
    if up:
        return [(k, k + 1) for k in range(count - 1)]
    return [(k + 1, k) for k in range(count - 1)]


def grow_both(cells, gate, axis, dim, widths):
    count = lax.axis_size(axis)
    lanes = gate.shape[-1]

    def ends(arr, width):
        size = arr.shape[dim]
        return lax.slice_in_dim(arr, 0, width, axis=dim), lax.slice_in_dim(arr, size - width, size, axis=dim)

    (cells_head, cells_tail), (gate_head, gate_tail) = ends(cells, widths[0]), ends(gate, widths[1])

    def pack(c, g):
        return jnp.concatenate([c.astype(jnp.float32).reshape(-1, lanes), g.reshape(-1, lanes)], 0)

    def unpack(m):
        split = cells_head.size // lanes
        return m[:split].reshape(cells_head.shape).astype(cells.dtype), m[split:].reshape(gate_head.shape)

    low = unpack(lax.ppermute(pack(cells_tail, gate_tail), axis, shift_pairs(count, True)))
    high = unpack(lax.ppermute(pack(cells_head, gate_head), axis, shift_pairs(count, False)))
    return (
        jnp.concatenate([low[0], cells, high[0]], axis=dim),
        jnp.concatenate([low[1], gate, high[1]], axis=dim),
    )


def grow(cells, axis, dim, width):
    count = lax.axis_size(axis)
    size = cells.shape[dim]
    head = lax.slice_in_dim(cells, 0, width, axis=dim)
    tail = lax.slice_in_dim(cells, size - width, size, axis=dim)
    low = lax.ppermute(tail, axis, shift_pairs(count, True))
    high = lax.ppermute(head, axis, shift_pairs(count, False))
    return jnp.concatenate([low, cells, high], axis=dim)


def body(
    coarse, coarse_mask, brick_live, field, coarse_weight, fine_weight_a, fine_weight_b, mod_weight
):
    channels = coarse_weight.shape[0]
    rows_x, rows_y, flat_z = coarse.shape
    cells_z = flat_z // channels
    edge = field.shape[0]
    half = edge // 2
    assert lax.axis_size("gz") == 2 and rows_x == half and 2 * rows_y == half and edge == 16
    lanes = 256
    zside = lax.axis_index("gz")
    first = zside == 0
    live = brick_live.reshape(())

    extra = jnp.concatenate(
        [
            coarse_mask.astype(jnp.bfloat16),
            jnp.broadcast_to(live.astype(jnp.bfloat16), (rows_x, rows_y, 1)),
            jnp.zeros((rows_x, rows_y, lanes - cells_z - 1), jnp.bfloat16),
        ],
        axis=2,
    )
    mine = jnp.concatenate([coarse, extra], axis=2)
    theirs = lax.ppermute(mine, "gz", [(0, 1), (1, 0)])
    column = jnp.where(first, jnp.concatenate([mine, theirs], 1), jnp.concatenate([theirs, mine], 1))
    live_other = theirs[0, 0, flat_z + cells_z]
    live_mine = live.astype(jnp.bfloat16)
    live_low = jnp.where(first, live_mine, live_other)
    live_high = jnp.where(first, live_other, live_mine)
    zcoarse = lax.broadcasted_iota(jnp.int32, (1, 1, cells_z), 2)
    live_z = jnp.where(zcoarse < half, live_low, live_high)
    keep = column[:, :, flat_z : flat_z + cells_z] * live_z
    packed = jnp.concatenate(
        [
            column[:, :, :flat_z],
            keep,
            jnp.zeros((rows_x, 2 * rows_y, lanes - cells_z), jnp.bfloat16),
        ],
        axis=2,
    )

    live_row = jnp.broadcast_to(live.astype(jnp.float32), (1, 128))
    gate_a, gate_b = gate_stage(field.reshape(edge * edge, -1), mod_weight, live_row)
    gate_a = gate_a.reshape(field.shape).transpose(1, 0, 2)
    width = edge * channels
    face = jnp.where(first, gate_a[:, :, width - channels :], gate_a[:, :, :channels])
    face = lax.ppermute(face, "gz", [(0, 1), (1, 0)])
    blank = jnp.zeros_like(face)
    gate_a = jnp.concatenate(
        [
            jnp.where(first, blank, face),
            gate_a,
            jnp.where(first, face, blank),
            jnp.zeros((edge, edge, 2 * channels), jnp.float32),
        ],
        axis=2,
    )
    region, gate_a = grow_both(packed, gate_a, "gy", 1, (2, 1))
    region, gate_a = grow_both(region, gate_a, "gx", 0, (2, 1))
    size = region.shape[0]
    volume = region[:, :, :flat_z].reshape(size, size, cells_z, channels)
    volume = jnp.pad(volume, ((0, 0), (0, 0), (2, 2), (0, 0)))
    volume = lax.dynamic_slice_in_dim(volume, zside * half, half + 4, axis=2)
    keep = jnp.pad(region[:, :, flat_z : flat_z + cells_z], ((0, 0), (0, 0), (2, 2)))
    keep = lax.dynamic_slice_in_dim(keep, zside * half + 1, half + 2, axis=2)[1:-1, 1:-1]
    activity = convolve(volume, coarse_weight)
    centre = volume[1:-1, 1:-1, 1:-1].astype(jnp.float32)
    hidden = ((centre + jax.nn.silu(activity)) * keep[..., None].astype(jnp.float32)).astype(
        jnp.bfloat16
    )
    cells = hidden.shape[0] * hidden.shape[1]
    hid = jnp.pad(hidden.reshape(cells, -1), ((0, ROWS_C - cells), (0, 0)))

    gate_a = jnp.pad(gate_a, ((0, 0), (0, STRIDE - edge - 2), (0, 0))).reshape(-1, gate_a.shape[2])

    rows = jnp.arange(ROWS_F)
    fx, fy = rows // STRIDE, rows % STRIDE
    inside = (fx < edge + 4) & (fy < edge + 4)
    source = (fx // 2) * (half + 2) + fy // 2
    spread = (inside[:, None] & (source[:, None] == jnp.arange(ROWS_C)[None, :])).astype(
        jnp.bfloat16
    )
    band_a, band_b = band_stage(fine_weight_a, fine_weight_b)
    out = fine_stage(hid, spread, gate_a, gate_b, band_a, band_b)
    return out.reshape(field.shape)


def solution(mesh):
    in_specs = (
        P(("groups", "gx"), ("gy", "gz"), None),
        P(("groups", "gx"), ("gy", "gz"), None),
        P(("groups", "gx"), "gy", "gz"),
        P(("groups", "gx"), "gy", "gz"),
        P(),
        P(),
        P(),
        P(),
    )
    out_specs = P(("groups", "gx"), "gy", "gz")
    return jax.shard_map(body, mesh=mesh, in_specs=in_specs, out_specs=out_specs, check_vma=False)
```

```python
import jax
import jax.numpy as jnp
from jax import lax
from jax.experimental import pallas as pl
from jax.experimental.pallas import tpu as pltpu
from jax.sharding import PartitionSpec as P

conv_layout = ("NDHWC", "DHWIO", "NDHWC")

STRIDE = 24
ROWS_C = 112
ROWS_F = 488
ROWS_A = 432
ROWS_B = 384
ROWS_L = 440
LANES_F = 1408
LANES_A = 1280
LANES_B = 1024


def select(shape, rule):
    rows = lax.broadcasted_iota(jnp.int32, shape, 0)
    cols = lax.broadcasted_iota(jnp.int32, shape, 1)
    return rule(rows, cols)


def build_bands(w_ref, band_ref):
    halves = [
        select((128, 256), lambda r, c, h=h: ((r >> 6) == h) & ((r & 63) == (c & 63))).astype(
            jnp.bfloat16
        )
        for h in range(2)
    ]
    column = select((64, 256), lambda r, c: c >> 6)
    for t in range(9):
        spreads = []
        for dz in range(3):
            d = 3 * t + dz
            low = 128 * (d // 2)
            high = min(low + 128, w_ref.shape[1])
            pick = halves[d % 2][: high - low]
            spreads.append(jnp.dot(w_ref[:, low:high], pick, preferred_element_type=jnp.float32))
        for zi in range(6):
            part = jnp.zeros((64, 256), jnp.float32)
            for dz in range(3):
                part = jnp.where(column == zi - dz, spreads[dz], part)
            band_ref[t, 64 * zi : 64 * zi + 64, :] = part.astype(jnp.bfloat16)


def gate_kernel(field_ref, mw_ref, live_ref, ga_ref, gb_ref):
    tiles = []
    for part in range(2):
        pick = select((128, 128), lambda r, c, p=part: ((r >> 6) == p) & ((r & 63) == (c & 63)))
        spread = jnp.dot(mw_ref[...], pick.astype(jnp.bfloat16), preferred_element_type=jnp.float32)
        rows_all = select((128, 64), lambda r, c: (r & 63) == c).astype(jnp.bfloat16)
        tall = jnp.dot(rows_all, spread.astype(jnp.bfloat16), preferred_element_type=jnp.float32)
        keep = select((128, 128), lambda r, c: (r >> 6) == (c >> 6))
        tiles.append(jnp.where(keep, tall, 0.0).astype(jnp.bfloat16))
    live = live_ref[...]
    for k in range(field_ref.shape[1] // 128):
        lanes = slice(128 * k, 128 * k + 128)
        x = field_ref[:, lanes]
        for tile, out in zip(tiles, (ga_ref, gb_ref)):
            v = jnp.dot(x, tile, preferred_element_type=jnp.float32)
            out[:, lanes] = live / (1.0 + jnp.exp(-v))


def gate_stage(field2d, mod_weight, live_row):
    shape = jax.ShapeDtypeStruct(field2d.shape, jnp.float32)
    return pl.pallas_call(gate_kernel, out_shape=(shape, shape))(field2d, mod_weight, live_row)


def silu(v):
    return v / (1.0 + jnp.exp(-v))


def band_kernel(w_raw, w_ref):
    build_bands(w_raw, w_ref)


def band_stage(weight):
    flops = 27 * 2 * 64 * 128 * 256
    return pl.pallas_call(
        band_kernel,
        out_shape=jax.ShapeDtypeStruct((9, 384, 256), jnp.bfloat16),
        cost_estimate=pl.CostEstimate(flops=flops, transcendentals=0, bytes_accessed=2 * 9 * 384 * 256),
    )(weight)


def fine_kernel(hid_ref, spread_ref, ga_ref, gb_ref, wa_ref, wb_ref, out_ref, fin_ref, lvl_ref):
    wide_c = hid_ref.shape[1]
    i = lax.broadcasted_iota(jnp.int32, (wide_c, LANES_F), 0)
    j = lax.broadcasted_iota(jnp.int32, (wide_c, LANES_F), 1)
    zup = (((i >> 6) == (j >> 7)) & ((i & 63) == (j & 63)) & (j < LANES_A)).astype(jnp.bfloat16)
    deep = jnp.dot(hid_ref[...], zup, preferred_element_type=jnp.float32).astype(jnp.bfloat16)
    fin_ref[...] = jnp.dot(spread_ref[...], deep, preferred_element_type=jnp.float32)
    r = lax.broadcasted_iota(jnp.int32, (384, 256), 0)
    c = lax.broadcasted_iota(jnp.int32, (384, 256), 1)
    shift = (r == c + 64).astype(jnp.bfloat16)
    lvl_ref[ROWS_A:, :] = jnp.zeros((ROWS_L - ROWS_A, LANES_A), jnp.float32)

    def conv(src, weights, rows, chunk):
        acc = jnp.zeros((rows, 256), jnp.float32)
        centre = None
        for t in range(9):
            dx, dy = divmod(t, 3)
            off = dx * STRIDE + dy
            a = src[off : off + rows, 256 * chunk : 256 * chunk + 384].astype(jnp.bfloat16)
            acc = acc + jnp.dot(a, weights[t], preferred_element_type=jnp.float32)
            if t == 4:
                centre = jnp.dot(a, shift, preferred_element_type=jnp.float32)
        return centre, acc

    for k in range(LANES_A // 256):
        centre, acc = conv(fin_ref, wa_ref, ROWS_A, k)
        lanes = slice(256 * k, 256 * k + 256)
        step = centre + silu(acc) * ga_ref[:, lanes]
        lvl_ref[:ROWS_A, lanes] = step.astype(jnp.bfloat16).astype(jnp.float32)
    for k in range(LANES_B // 256):
        centre, acc = conv(lvl_ref, wb_ref, ROWS_B, k)
        lanes = slice(256 * k, 256 * k + 256)
        edge = out_ref.shape[0] // 16
        for x in range(edge):
            mine = slice(x * STRIDE, x * STRIDE + 16)
            value = centre[mine] + silu(acc[mine]) * gb_ref[16 * x : 16 * x + 16, lanes]
            out_ref[16 * x : 16 * x + 16, lanes] = value.astype(out_ref.dtype)


def fine_stage(hid, spread, gate_a, gate_b, band_a, band_b):
    return pl.pallas_call(
        fine_kernel,
        out_shape=jax.ShapeDtypeStruct(gate_b.shape, jnp.bfloat16),
        scratch_shapes=[
            pltpu.VMEM((ROWS_F, LANES_F), jnp.float32),
            pltpu.VMEM((ROWS_L, LANES_A), jnp.float32),
        ],
    )(hid, spread, gate_a, gate_b, band_a, band_b)


def convolve(padded, weight):
    channels = weight.shape[0]
    kernel = weight.reshape(channels, 3, 3, 3, channels).transpose(1, 2, 3, 0, 4)
    result = lax.conv_general_dilated(
        padded[None],
        kernel,
        (1, 1, 1),
        "VALID",
        dimension_numbers=conv_layout,
        preferred_element_type=jnp.float32,
    )
    return result[0]


def shift_pairs(count, up):
    if up:
        return [(k, k + 1) for k in range(count - 1)]
    return [(k + 1, k) for k in range(count - 1)]


def grow_both(cells, gate, axis, dim, widths):
    count = lax.axis_size(axis)
    lanes = gate.shape[-1]

    def ends(arr, width):
        size = arr.shape[dim]
        return lax.slice_in_dim(arr, 0, width, axis=dim), lax.slice_in_dim(arr, size - width, size, axis=dim)

    (cells_head, cells_tail), (gate_head, gate_tail) = ends(cells, widths[0]), ends(gate, widths[1])

    def pack(c, g):
        return jnp.concatenate([c.astype(jnp.float32).reshape(-1, lanes), g.reshape(-1, lanes)], 0)

    def unpack(m):
        split = cells_head.size // lanes
        return m[:split].reshape(cells_head.shape).astype(cells.dtype), m[split:].reshape(gate_head.shape)

    low = unpack(lax.ppermute(pack(cells_tail, gate_tail), axis, shift_pairs(count, True)))
    high = unpack(lax.ppermute(pack(cells_head, gate_head), axis, shift_pairs(count, False)))
    return (
        jnp.concatenate([low[0], cells, high[0]], axis=dim),
        jnp.concatenate([low[1], gate, high[1]], axis=dim),
    )


def grow(cells, axis, dim, width):
    count = lax.axis_size(axis)
    size = cells.shape[dim]
    head = lax.slice_in_dim(cells, 0, width, axis=dim)
    tail = lax.slice_in_dim(cells, size - width, size, axis=dim)
    low = lax.ppermute(tail, axis, shift_pairs(count, True))
    high = lax.ppermute(head, axis, shift_pairs(count, False))
    return jnp.concatenate([low, cells, high], axis=dim)


def body(
    coarse, coarse_mask, brick_live, field, coarse_weight, fine_weight_a, fine_weight_b, mod_weight
):
    channels = coarse_weight.shape[0]
    rows_x, rows_y, flat_z = coarse.shape
    cells_z = flat_z // channels
    edge = field.shape[0]
    half = edge // 2
    assert lax.axis_size("gz") == 2 and rows_x == half and 2 * rows_y == half
    lanes = 256
    zside = lax.axis_index("gz")
    first = zside == 0
    live = brick_live.reshape(())

    extra = jnp.concatenate(
        [
            coarse_mask.astype(jnp.bfloat16),
            jnp.broadcast_to(live.astype(jnp.bfloat16), (rows_x, rows_y, 1)),
            jnp.zeros((rows_x, rows_y, lanes - cells_z - 1), jnp.bfloat16),
        ],
        axis=2,
    )
    mine = jnp.concatenate([coarse, extra], axis=2)
    theirs = lax.ppermute(mine, "gz", [(0, 1), (1, 0)])
    column = jnp.where(first, jnp.concatenate([mine, theirs], 1), jnp.concatenate([theirs, mine], 1))
    live_other = theirs[0, 0, flat_z + cells_z]
    live_mine = live.astype(jnp.bfloat16)
    live_low = jnp.where(first, live_mine, live_other)
    live_high = jnp.where(first, live_other, live_mine)
    zcoarse = lax.broadcasted_iota(jnp.int32, (1, 1, cells_z), 2)
    live_z = jnp.where(zcoarse < half, live_low, live_high)
    keep = column[:, :, flat_z : flat_z + cells_z] * live_z
    packed = jnp.concatenate(
        [
            column[:, :, :flat_z],
            keep,
            jnp.zeros((rows_x, 2 * rows_y, lanes - cells_z), jnp.bfloat16),
        ],
        axis=2,
    )

    live_row = jnp.broadcast_to(live.astype(jnp.float32), (1, 128))
    gate_a, gate_b = gate_stage(field.reshape(edge * edge, -1), mod_weight, live_row)
    gate_a = gate_a.reshape(field.shape)
    width = edge * channels
    face = jnp.where(first, gate_a[:, :, width - channels :], gate_a[:, :, :channels])
    face = lax.ppermute(face, "gz", [(0, 1), (1, 0)])
    blank = jnp.zeros_like(face)
    gate_a = jnp.concatenate(
        [
            jnp.where(first, blank, face),
            gate_a,
            jnp.where(first, face, blank),
            jnp.zeros((edge, edge, 2 * channels), jnp.float32),
        ],
        axis=2,
    )
    region, gate_a = grow_both(packed, gate_a, "gy", 1, (2, 1))
    late_weight, region = lax.optimization_barrier((fine_weight_b, region))
    region, gate_a = grow_both(region, gate_a, "gx", 0, (2, 1))
    size = region.shape[0]
    volume = region[:, :, :flat_z].reshape(size, size, cells_z, channels)
    volume = jnp.pad(volume, ((0, 0), (0, 0), (2, 2), (0, 0)))
    volume = lax.dynamic_slice_in_dim(volume, zside * half, half + 4, axis=2)
    keep = jnp.pad(region[:, :, flat_z : flat_z + cells_z], ((0, 0), (0, 0), (2, 2)))
    keep = lax.dynamic_slice_in_dim(keep, zside * half + 1, half + 2, axis=2)[1:-1, 1:-1]
    activity = convolve(volume, coarse_weight)
    centre = volume[1:-1, 1:-1, 1:-1].astype(jnp.float32)
    hidden = ((centre + jax.nn.silu(activity)) * keep[..., None].astype(jnp.float32)).astype(
        jnp.bfloat16
    )
    cells = hidden.shape[0] * hidden.shape[1]
    hid = jnp.pad(hidden.reshape(cells, -1), ((0, ROWS_C - cells), (0, 0)))

    gate_a = jnp.pad(gate_a, ((0, 0), (0, STRIDE - edge - 2), (0, 0))).reshape(-1, gate_a.shape[2])

    rows = jnp.arange(ROWS_F)
    fx, fy = rows // STRIDE, rows % STRIDE
    inside = (fx < edge + 4) & (fy < edge + 4)
    source = (fx // 2) * (half + 2) + fy // 2
    spread = (inside[:, None] & (source[:, None] == jnp.arange(ROWS_C)[None, :])).astype(
        jnp.bfloat16
    )
    band_a, band_b = band_stage(fine_weight_a), band_stage(late_weight)
    out = fine_stage(hid, spread, gate_a, gate_b, band_a, band_b)
    return out.reshape(field.shape)


def solution(mesh):
    in_specs = (
        P(("groups", "gx"), ("gy", "gz"), None),
        P(("groups", "gx"), ("gy", "gz"), None),
        P(("groups", "gx"), "gy", "gz"),
        P(("groups", "gx"), "gy", "gz"),
        P(),
        P(),
        P(),
        P(),
    )
    out_specs = P(("groups", "gx"), "gy", "gz")
    return jax.shard_map(body, mesh=mesh, in_specs=in_specs, out_specs=out_specs, check_vma=False)
```

```python
import jax
import jax.numpy as jnp
from jax import lax
from jax.experimental import pallas as pl
from jax.experimental.pallas import tpu as pltpu
from jax.sharding import PartitionSpec as P

conv_layout = ("NDHWC", "DHWIO", "NDHWC")

STRIDE = 24
ROWS_C = 112
ROWS_F = 488
ROWS_A = 432
ROWS_B = 384
ROWS_L = 440
LANES_F = 1408
LANES_A = 1280
LANES_B = 1024


def select(shape, rule):
    rows = lax.broadcasted_iota(jnp.int32, shape, 0)
    cols = lax.broadcasted_iota(jnp.int32, shape, 1)
    return rule(rows, cols)


def build_bands(w_ref, band_ref):
    halves = [
        select((128, 256), lambda r, c, h=h: ((r >> 6) == h) & ((r & 63) == (c & 63))).astype(
            jnp.bfloat16
        )
        for h in range(2)
    ]
    column = select((64, 256), lambda r, c: c >> 6)
    for t in range(9):
        spreads = []
        for dz in range(3):
            d = 3 * t + dz
            low = 128 * (d // 2)
            high = min(low + 128, w_ref.shape[1])
            pick = halves[d % 2][: high - low]
            spreads.append(jnp.dot(w_ref[:, low:high], pick, preferred_element_type=jnp.float32))
        for zi in range(6):
            part = jnp.zeros((64, 256), jnp.float32)
            for dz in range(3):
                part = jnp.where(column == zi - dz, spreads[dz], part)
            band_ref[t, 64 * zi : 64 * zi + 64, :] = part.astype(jnp.bfloat16)


def gate_kernel(field_ref, mw_ref, live_ref, ga_ref, gb_ref):
    tiles = []
    for part in range(2):
        pick = select((128, 128), lambda r, c, p=part: ((r >> 6) == p) & ((r & 63) == (c & 63)))
        spread = jnp.dot(mw_ref[...], pick.astype(jnp.bfloat16), preferred_element_type=jnp.float32)
        rows_all = select((128, 64), lambda r, c: (r & 63) == c).astype(jnp.bfloat16)
        tall = jnp.dot(rows_all, spread.astype(jnp.bfloat16), preferred_element_type=jnp.float32)
        keep = select((128, 128), lambda r, c: (r >> 6) == (c >> 6))
        tiles.append(jnp.where(keep, tall, 0.0).astype(jnp.bfloat16))
    live = live_ref[...]
    for k in range(field_ref.shape[1] // 128):
        lanes = slice(128 * k, 128 * k + 128)
        x = field_ref[:, lanes]
        for tile, out in zip(tiles, (ga_ref, gb_ref)):
            v = jnp.dot(x, tile, preferred_element_type=jnp.float32)
            out[:, lanes] = live / (1.0 + jnp.exp(-v))


def gate_stage(field2d, mod_weight, live_row):
    shape = jax.ShapeDtypeStruct(field2d.shape, jnp.float32)
    return pl.pallas_call(gate_kernel, out_shape=(shape, shape))(field2d, mod_weight, live_row)


def silu(v):
    return v / (1.0 + jnp.exp(-v))


def band_kernel(wa_raw, wb_raw, wa_ref, wb_ref):
    build_bands(wa_raw, wa_ref)
    build_bands(wb_raw, wb_ref)


def band_stage(weight_a, weight_b):
    shape = jax.ShapeDtypeStruct((9, 384, 256), jnp.bfloat16)
    flops = 2 * 27 * 2 * (64 * 128 * 256 + 384 * 64 * 256)
    return pl.pallas_call(
        band_kernel,
        out_shape=(shape, shape),
        cost_estimate=pl.CostEstimate(flops=flops, transcendentals=0, bytes_accessed=4 * 9 * 384 * 256),
    )(weight_a, weight_b)


def fine_kernel(hid_ref, spread_ref, ga_ref, gb_ref, wa_ref, wb_ref, out_ref, fin_ref, lvl_ref):
    wide_c = hid_ref.shape[1]
    i = lax.broadcasted_iota(jnp.int32, (wide_c, LANES_F), 0)
    j = lax.broadcasted_iota(jnp.int32, (wide_c, LANES_F), 1)
    zup = (((i >> 6) == (j >> 7)) & ((i & 63) == (j & 63)) & (j < LANES_A)).astype(jnp.bfloat16)
    deep = jnp.dot(hid_ref[...], zup, preferred_element_type=jnp.float32).astype(jnp.bfloat16)
    fin_ref[...] = jnp.dot(spread_ref[...], deep, preferred_element_type=jnp.float32)
    r = lax.broadcasted_iota(jnp.int32, (384, 256), 0)
    c = lax.broadcasted_iota(jnp.int32, (384, 256), 1)
    shift = (r == c + 64).astype(jnp.bfloat16)
    lvl_ref[ROWS_A:, :] = jnp.zeros((ROWS_L - ROWS_A, LANES_A), jnp.float32)

    def conv(src, weights, rows, chunk, cells=4):
        acc = jnp.zeros((rows, 64 * cells), jnp.float32)
        centre = None
        for t in range(9):
            dx, dy = divmod(t, 3)
            off = dx * STRIDE + dy
            a = src[off : off + rows, 256 * chunk : 256 * chunk + 64 * cells + 128]
            a = a.astype(jnp.bfloat16)
            band = weights[t, : 64 * cells + 128, : 64 * cells]
            acc = acc + jnp.dot(a, band, preferred_element_type=jnp.float32)
            if t == 4:
                picked = shift[: 64 * cells + 128, : 64 * cells]
                centre = jnp.dot(a, picked, preferred_element_type=jnp.float32)
        return centre, acc

    for k in range(LANES_A // 256):
        cells = 4 if k < LANES_A // 256 - 1 else 2
        centre, acc = conv(fin_ref, wa_ref, ROWS_A, k, cells)
        lanes = slice(256 * k, 256 * k + 64 * cells)
        step = centre + silu(acc) * ga_ref[:, lanes]
        lvl_ref[:ROWS_A, lanes] = step.astype(jnp.bfloat16).astype(jnp.float32)
    for k in range(LANES_B // 256):
        centre, acc = conv(lvl_ref, wb_ref, ROWS_B, k)
        lanes = slice(256 * k, 256 * k + 256)
        edge = out_ref.shape[0] // 16
        for x in range(edge):
            mine = slice(x * STRIDE, x * STRIDE + 16)
            value = centre[mine] + silu(acc[mine]) * gb_ref[16 * x : 16 * x + 16, lanes]
            out_ref[16 * x : 16 * x + 16, lanes] = value.astype(out_ref.dtype)


def fine_stage(hid, spread, gate_a, gate_b, band_a, band_b):
    return pl.pallas_call(
        fine_kernel,
        out_shape=jax.ShapeDtypeStruct(gate_b.shape, jnp.bfloat16),
        scratch_shapes=[
            pltpu.VMEM((ROWS_F, LANES_F), jnp.float32),
            pltpu.VMEM((ROWS_L, LANES_A), jnp.float32),
        ],
    )(hid, spread, gate_a, gate_b, band_a, band_b)


def convolve(padded, weight):
    channels = weight.shape[0]
    kernel = weight.reshape(channels, 3, 3, 3, channels).transpose(1, 2, 3, 0, 4)
    result = lax.conv_general_dilated(
        padded[None],
        kernel,
        (1, 1, 1),
        "VALID",
        dimension_numbers=conv_layout,
        preferred_element_type=jnp.float32,
    )
    return result[0]


def shift_pairs(count, up):
    if up:
        return [(k, k + 1) for k in range(count - 1)]
    return [(k + 1, k) for k in range(count - 1)]


def grow_both(cells, gate, axis, dim, widths):
    count = lax.axis_size(axis)
    lanes = gate.shape[-1]

    def ends(arr, width):
        size = arr.shape[dim]
        return lax.slice_in_dim(arr, 0, width, axis=dim), lax.slice_in_dim(arr, size - width, size, axis=dim)

    (cells_head, cells_tail), (gate_head, gate_tail) = ends(cells, widths[0]), ends(gate, widths[1])

    def pack(c, g):
        return jnp.concatenate([c.astype(jnp.float32).reshape(-1, lanes), g.reshape(-1, lanes)], 0)

    def unpack(m):
        split = cells_head.size // lanes
        return m[:split].reshape(cells_head.shape).astype(cells.dtype), m[split:].reshape(gate_head.shape)

    low = unpack(lax.ppermute(pack(cells_tail, gate_tail), axis, shift_pairs(count, True)))
    high = unpack(lax.ppermute(pack(cells_head, gate_head), axis, shift_pairs(count, False)))
    return (
        jnp.concatenate([low[0], cells, high[0]], axis=dim),
        jnp.concatenate([low[1], gate, high[1]], axis=dim),
    )


def grow(cells, axis, dim, width):
    count = lax.axis_size(axis)
    size = cells.shape[dim]
    head = lax.slice_in_dim(cells, 0, width, axis=dim)
    tail = lax.slice_in_dim(cells, size - width, size, axis=dim)
    low = lax.ppermute(tail, axis, shift_pairs(count, True))
    high = lax.ppermute(head, axis, shift_pairs(count, False))
    return jnp.concatenate([low, cells, high], axis=dim)


def body(
    coarse, coarse_mask, brick_live, field, coarse_weight, fine_weight_a, fine_weight_b, mod_weight
):
    channels = coarse_weight.shape[0]
    rows_x, rows_y, flat_z = coarse.shape
    cells_z = flat_z // channels
    edge = field.shape[0]
    half = edge // 2
    assert lax.axis_size("gz") == 2 and rows_x == half and 2 * rows_y == half
    lanes = 256
    zside = lax.axis_index("gz")
    first = zside == 0
    live = brick_live.reshape(())

    extra = jnp.concatenate(
        [
            coarse_mask.astype(jnp.bfloat16),
            jnp.broadcast_to(live.astype(jnp.bfloat16), (rows_x, rows_y, 1)),
            jnp.zeros((rows_x, rows_y, lanes - cells_z - 1), jnp.bfloat16),
        ],
        axis=2,
    )
    mine = jnp.concatenate([coarse, extra], axis=2)
    theirs = lax.ppermute(mine, "gz", [(0, 1), (1, 0)])
    column = jnp.where(first, jnp.concatenate([mine, theirs], 1), jnp.concatenate([theirs, mine], 1))
    live_other = theirs[0, 0, flat_z + cells_z]
    live_mine = live.astype(jnp.bfloat16)
    live_low = jnp.where(first, live_mine, live_other)
    live_high = jnp.where(first, live_other, live_mine)
    zcoarse = lax.broadcasted_iota(jnp.int32, (1, 1, cells_z), 2)
    live_z = jnp.where(zcoarse < half, live_low, live_high)
    keep = column[:, :, flat_z : flat_z + cells_z] * live_z
    packed = jnp.concatenate(
        [
            column[:, :, :flat_z],
            keep,
            jnp.zeros((rows_x, 2 * rows_y, lanes - cells_z), jnp.bfloat16),
        ],
        axis=2,
    )

    live_row = jnp.broadcast_to(live.astype(jnp.float32), (1, 128))
    gate_a, gate_b = gate_stage(field.reshape(edge * edge, -1), mod_weight, live_row)
    gate_a = gate_a.reshape(field.shape)
    width = edge * channels
    face = jnp.where(first, gate_a[:, :, width - channels :], gate_a[:, :, :channels])
    face = lax.ppermute(face, "gz", [(0, 1), (1, 0)])
    blank = jnp.zeros_like(face)
    gate_a = jnp.concatenate(
        [
            jnp.where(first, blank, face),
            gate_a,
            jnp.where(first, face, blank),
            jnp.zeros((edge, edge, 2 * channels), jnp.float32),
        ],
        axis=2,
    )
    region, gate_a = grow_both(packed, gate_a, "gy", 1, (2, 1))
    region, gate_a = grow_both(region, gate_a, "gx", 0, (2, 1))
    size = region.shape[0]
    volume = region[:, :, :flat_z].reshape(size, size, cells_z, channels)
    volume = jnp.pad(volume, ((0, 0), (0, 0), (2, 2), (0, 0)))
    volume = lax.dynamic_slice_in_dim(volume, zside * half, half + 4, axis=2)
    keep = jnp.pad(region[:, :, flat_z : flat_z + cells_z], ((0, 0), (0, 0), (2, 2)))
    keep = lax.dynamic_slice_in_dim(keep, zside * half + 1, half + 2, axis=2)[1:-1, 1:-1]
    activity = convolve(volume, coarse_weight)
    centre = volume[1:-1, 1:-1, 1:-1].astype(jnp.float32)
    hidden = ((centre + jax.nn.silu(activity)) * keep[..., None].astype(jnp.float32)).astype(
        jnp.bfloat16
    )
    cells = hidden.shape[0] * hidden.shape[1]
    hid = jnp.pad(hidden.reshape(cells, -1), ((0, ROWS_C - cells), (0, 0)))

    gate_a = jnp.pad(gate_a, ((0, 0), (0, STRIDE - edge - 2), (0, 0))).reshape(-1, gate_a.shape[2])

    rows = jnp.arange(ROWS_F)
    fx, fy = rows // STRIDE, rows % STRIDE
    inside = (fx < edge + 4) & (fy < edge + 4)
    source = (fx // 2) * (half + 2) + fy // 2
    spread = (inside[:, None] & (source[:, None] == jnp.arange(ROWS_C)[None, :])).astype(
        jnp.bfloat16
    )
    band_a, band_b = band_stage(fine_weight_a, fine_weight_b)
    out = fine_stage(hid, spread, gate_a, gate_b, band_a, band_b)
    return out.reshape(field.shape)


def solution(mesh):
    in_specs = (
        P(("groups", "gx"), ("gy", "gz"), None),
        P(("groups", "gx"), ("gy", "gz"), None),
        P(("groups", "gx"), "gy", "gz"),
        P(("groups", "gx"), "gy", "gz"),
        P(),
        P(),
        P(),
        P(),
    )
    out_specs = P(("groups", "gx"), "gy", "gz")
    return jax.shard_map(body, mesh=mesh, in_specs=in_specs, out_specs=out_specs, check_vma=False)
```

```python
import jax
import jax.numpy as jnp
from jax import lax
from jax.experimental import pallas as pl
from jax.experimental.pallas import tpu as pltpu
from jax.sharding import PartitionSpec as P

conv_layout = ("NDHWC", "DHWIO", "NDHWC")

STRIDE = 24
ROWS_C = 112
ROWS_F = 488
ROWS_A = 432
ROWS_B = 384
ROWS_L = 440
LANES_F = 1280
LANES_A = 1280
LANES_B = 1024


def select(shape, rule):
    rows = lax.broadcasted_iota(jnp.int32, shape, 0)
    cols = lax.broadcasted_iota(jnp.int32, shape, 1)
    return rule(rows, cols)


def build_bands(w_ref, band_ref):
    halves = [
        select((128, 256), lambda r, c, h=h: ((r >> 6) == h) & ((r & 63) == (c & 63))).astype(
            jnp.bfloat16
        )
        for h in range(2)
    ]
    column = select((64, 256), lambda r, c: c >> 6)
    for t in range(9):
        spreads = []
        for dz in range(3):
            d = 3 * t + dz
            low = 128 * (d // 2)
            high = min(low + 128, w_ref.shape[1])
            pick = halves[d % 2][: high - low]
            spreads.append(jnp.dot(w_ref[:, low:high], pick, preferred_element_type=jnp.float32))
        for zi in range(6):
            part = jnp.zeros((64, 256), jnp.float32)
            for dz in range(3):
                part = jnp.where(column == zi - dz, spreads[dz], part)
            band_ref[t, 64 * zi : 64 * zi + 64, :] = part.astype(jnp.bfloat16)


def gate_kernel(field_ref, mw_ref, live_ref, ga_ref, gb_ref):
    tiles = []
    for part in range(2):
        pick = select((128, 128), lambda r, c, p=part: ((r >> 6) == p) & ((r & 63) == (c & 63)))
        spread = jnp.dot(mw_ref[...], pick.astype(jnp.bfloat16), preferred_element_type=jnp.float32)
        rows_all = select((128, 64), lambda r, c: (r & 63) == c).astype(jnp.bfloat16)
        tall = jnp.dot(rows_all, spread.astype(jnp.bfloat16), preferred_element_type=jnp.float32)
        keep = select((128, 128), lambda r, c: (r >> 6) == (c >> 6))
        tiles.append(jnp.where(keep, tall, 0.0).astype(jnp.bfloat16))
    live = live_ref[...]
    for k in range(field_ref.shape[1] // 128):
        lanes = slice(128 * k, 128 * k + 128)
        x = field_ref[:, lanes]
        for tile, out in zip(tiles, (ga_ref, gb_ref)):
            v = jnp.dot(x, tile, preferred_element_type=jnp.float32)
            out[:, lanes] = live / (1.0 + jnp.exp(-v))


def gate_stage(field2d, mod_weight, live_row):
    shape = jax.ShapeDtypeStruct(field2d.shape, jnp.float32)
    return pl.pallas_call(gate_kernel, out_shape=(shape, shape))(field2d, mod_weight, live_row)


def silu(v):
    return v / (1.0 + jnp.exp(-v))


def band_kernel(wa_raw, wb_raw, wa_ref, wb_ref):
    build_bands(wa_raw, wa_ref)
    build_bands(wb_raw, wb_ref)


def band_stage(weight_a, weight_b):
    shape = jax.ShapeDtypeStruct((9, 384, 256), jnp.bfloat16)
    flops = 2 * 27 * 2 * (64 * 128 * 256 + 384 * 64 * 256)
    return pl.pallas_call(
        band_kernel,
        out_shape=(shape, shape),
        cost_estimate=pl.CostEstimate(flops=flops, transcendentals=0, bytes_accessed=4 * 9 * 384 * 256),
    )(weight_a, weight_b)


def fine_kernel(hid_ref, spread_ref, ga_ref, gb_ref, wa_ref, wb_ref, out_ref, fin_ref, lvl_ref):
    wide_c = hid_ref.shape[1]
    i = lax.broadcasted_iota(jnp.int32, (wide_c, LANES_F), 0)
    j = lax.broadcasted_iota(jnp.int32, (wide_c, LANES_F), 1)
    zup = (((i >> 6) == (j >> 7)) & ((i & 63) == (j & 63)) & (j < LANES_A)).astype(jnp.bfloat16)
    deep = jnp.dot(hid_ref[...], zup, preferred_element_type=jnp.float32).astype(jnp.bfloat16)
    fin_ref[...] = jnp.dot(spread_ref[...], deep, preferred_element_type=jnp.float32)
    r = lax.broadcasted_iota(jnp.int32, (384, 256), 0)
    c = lax.broadcasted_iota(jnp.int32, (384, 256), 1)
    shift = (r == c + 64).astype(jnp.bfloat16)
    lvl_ref[ROWS_A:, :] = jnp.zeros((ROWS_L - ROWS_A, LANES_A), jnp.float32)

    def conv(src, weights, rows, chunk, cells=4):
        acc = jnp.zeros((rows, 64 * cells), jnp.float32)
        centre = None
        for t in range(9):
            dx, dy = divmod(t, 3)
            off = dx * STRIDE + dy
            a = src[off : off + rows, 256 * chunk : 256 * chunk + 64 * cells + 128]
            a = a.astype(jnp.bfloat16)
            band = weights[t, : 64 * cells + 128, : 64 * cells]
            acc = acc + jnp.dot(a, band, preferred_element_type=jnp.float32)
            if t == 4:
                picked = shift[: 64 * cells + 128, : 64 * cells]
                centre = jnp.dot(a, picked, preferred_element_type=jnp.float32)
        return centre, acc

    for k in range(LANES_A // 256):
        cells = 4 if k < LANES_A // 256 - 1 else 2
        centre, acc = conv(fin_ref, wa_ref, ROWS_A, k, cells)
        lanes = slice(256 * k, 256 * k + 64 * cells)
        step = centre + silu(acc) * ga_ref[:, lanes]
        lvl_ref[:ROWS_A, lanes] = step.astype(jnp.bfloat16).astype(jnp.float32)
    for k in range(LANES_B // 256):
        centre, acc = conv(lvl_ref, wb_ref, ROWS_B, k)
        lanes = slice(256 * k, 256 * k + 256)
        edge = out_ref.shape[0] // 16
        for x in range(edge):
            mine = slice(x * STRIDE, x * STRIDE + 16)
            value = centre[mine] + silu(acc[mine]) * gb_ref[16 * x : 16 * x + 16, lanes]
            out_ref[16 * x : 16 * x + 16, lanes] = value.astype(out_ref.dtype)


def fine_stage(hid, spread, gate_a, gate_b, band_a, band_b):
    return pl.pallas_call(
        fine_kernel,
        out_shape=jax.ShapeDtypeStruct(gate_b.shape, jnp.bfloat16),
        scratch_shapes=[
            pltpu.VMEM((ROWS_F, LANES_F), jnp.float32),
            pltpu.VMEM((ROWS_L, LANES_A), jnp.float32),
        ],
    )(hid, spread, gate_a, gate_b, band_a, band_b)


def convolve(padded, weight):
    channels = weight.shape[0]
    kernel = weight.reshape(channels, 3, 3, 3, channels).transpose(1, 2, 3, 0, 4)
    result = lax.conv_general_dilated(
        padded[None],
        kernel,
        (1, 1, 1),
        "VALID",
        dimension_numbers=conv_layout,
        preferred_element_type=jnp.float32,
    )
    return result[0]


def shift_pairs(count, up):
    if up:
        return [(k, k + 1) for k in range(count - 1)]
    return [(k + 1, k) for k in range(count - 1)]


def grow_both(cells, gate, axis, dim, widths):
    count = lax.axis_size(axis)
    lanes = gate.shape[-1]

    def ends(arr, width):
        size = arr.shape[dim]
        return lax.slice_in_dim(arr, 0, width, axis=dim), lax.slice_in_dim(arr, size - width, size, axis=dim)

    (cells_head, cells_tail), (gate_head, gate_tail) = ends(cells, widths[0]), ends(gate, widths[1])

    def pack(c, g):
        return jnp.concatenate([c.astype(jnp.float32).reshape(-1, lanes), g.reshape(-1, lanes)], 0)

    def unpack(m):
        split = cells_head.size // lanes
        return m[:split].reshape(cells_head.shape).astype(cells.dtype), m[split:].reshape(gate_head.shape)

    low = unpack(lax.ppermute(pack(cells_tail, gate_tail), axis, shift_pairs(count, True)))
    high = unpack(lax.ppermute(pack(cells_head, gate_head), axis, shift_pairs(count, False)))
    return (
        jnp.concatenate([low[0], cells, high[0]], axis=dim),
        jnp.concatenate([low[1], gate, high[1]], axis=dim),
    )


def grow(cells, axis, dim, width):
    count = lax.axis_size(axis)
    size = cells.shape[dim]
    head = lax.slice_in_dim(cells, 0, width, axis=dim)
    tail = lax.slice_in_dim(cells, size - width, size, axis=dim)
    low = lax.ppermute(tail, axis, shift_pairs(count, True))
    high = lax.ppermute(head, axis, shift_pairs(count, False))
    return jnp.concatenate([low, cells, high], axis=dim)


def body(
    coarse, coarse_mask, brick_live, field, coarse_weight, fine_weight_a, fine_weight_b, mod_weight
):
    channels = coarse_weight.shape[0]
    rows_x, rows_y, flat_z = coarse.shape
    cells_z = flat_z // channels
    edge = field.shape[0]
    half = edge // 2
    assert lax.axis_size("gz") == 2 and rows_x == half and 2 * rows_y == half
    lanes = 256
    zside = lax.axis_index("gz")
    first = zside == 0
    live = brick_live.reshape(())

    extra = jnp.concatenate(
        [
            coarse_mask.astype(jnp.bfloat16),
            jnp.broadcast_to(live.astype(jnp.bfloat16), (rows_x, rows_y, 1)),
            jnp.zeros((rows_x, rows_y, lanes - cells_z - 1), jnp.bfloat16),
        ],
        axis=2,
    )
    mine = jnp.concatenate([coarse, extra], axis=2)
    theirs = lax.ppermute(mine, "gz", [(0, 1), (1, 0)])
    column = jnp.where(first, jnp.concatenate([mine, theirs], 1), jnp.concatenate([theirs, mine], 1))
    live_other = theirs[0, 0, flat_z + cells_z]
    live_mine = live.astype(jnp.bfloat16)
    live_low = jnp.where(first, live_mine, live_other)
    live_high = jnp.where(first, live_other, live_mine)
    zcoarse = lax.broadcasted_iota(jnp.int32, (1, 1, cells_z), 2)
    live_z = jnp.where(zcoarse < half, live_low, live_high)
    keep = column[:, :, flat_z : flat_z + cells_z] * live_z
    packed = jnp.concatenate(
        [
            column[:, :, :flat_z],
            keep,
            jnp.zeros((rows_x, 2 * rows_y, lanes - cells_z), jnp.bfloat16),
        ],
        axis=2,
    )

    live_row = jnp.broadcast_to(live.astype(jnp.float32), (1, 128))
    gate_a, gate_b = gate_stage(field.reshape(edge * edge, -1), mod_weight, live_row)
    gate_a = gate_a.reshape(field.shape)
    width = edge * channels
    face = jnp.where(first, gate_a[:, :, width - channels :], gate_a[:, :, :channels])
    face = lax.ppermute(face, "gz", [(0, 1), (1, 0)])
    blank = jnp.zeros_like(face)
    gate_a = jnp.concatenate(
        [
            jnp.where(first, blank, face),
            gate_a,
            jnp.where(first, face, blank),
            jnp.zeros((edge, edge, 2 * channels), jnp.float32),
        ],
        axis=2,
    )
    region, gate_a = grow_both(packed, gate_a, "gy", 1, (2, 1))
    region, gate_a = grow_both(region, gate_a, "gx", 0, (2, 1))
    size = region.shape[0]
    volume = region[:, :, :flat_z].reshape(size, size, cells_z, channels)
    volume = jnp.pad(volume, ((0, 0), (0, 0), (2, 2), (0, 0)))
    volume = lax.dynamic_slice_in_dim(volume, zside * half, half + 4, axis=2)
    keep = jnp.pad(region[:, :, flat_z : flat_z + cells_z], ((0, 0), (0, 0), (2, 2)))
    keep = lax.dynamic_slice_in_dim(keep, zside * half + 1, half + 2, axis=2)[1:-1, 1:-1]
    activity = convolve(volume, coarse_weight)
    centre = volume[1:-1, 1:-1, 1:-1].astype(jnp.float32)
    hidden = ((centre + jax.nn.silu(activity)) * keep[..., None].astype(jnp.float32)).astype(
        jnp.bfloat16
    )
    cells = hidden.shape[0] * hidden.shape[1]
    hid = jnp.pad(hidden.reshape(cells, -1), ((0, ROWS_C - cells), (0, 0)))

    gate_a = jnp.pad(gate_a, ((0, 0), (0, STRIDE - edge - 2), (0, 0))).reshape(-1, gate_a.shape[2])

    rows = jnp.arange(ROWS_F)
    fx, fy = rows // STRIDE, rows % STRIDE
    inside = (fx < edge + 4) & (fy < edge + 4)
    source = (fx // 2) * (half + 2) + fy // 2
    spread = (inside[:, None] & (source[:, None] == jnp.arange(ROWS_C)[None, :])).astype(
        jnp.bfloat16
    )
    band_a, band_b = band_stage(fine_weight_a, fine_weight_b)
    out = fine_stage(hid, spread, gate_a, gate_b, band_a, band_b)
    return out.reshape(field.shape)


def solution(mesh):
    in_specs = (
        P(("groups", "gx"), ("gy", "gz"), None),
        P(("groups", "gx"), ("gy", "gz"), None),
        P(("groups", "gx"), "gy", "gz"),
        P(("groups", "gx"), "gy", "gz"),
        P(),
        P(),
        P(),
        P(),
    )
    out_specs = P(("groups", "gx"), "gy", "gz")
    return jax.shard_map(body, mesh=mesh, in_specs=in_specs, out_specs=out_specs, check_vma=False)
```
